256 devices in a mesh: depth: 8 (over y_hi, x), shots: 32 (over z, y_lo, core).
Axes of the slice: x: 4, y: 4 (y_hi: 2, y_lo: 2; y = y_hi * 2 + y_lo), z: 8, core: 2. Of those that a mesh axis runs over, the one named last changes fastest.
Arguments:
- adj_now: float32 [32, 128, 128, 128], P('shots', 'depth'), may hold values from -6 to 6
- adj_prev: float32 [32, 128, 128, 128], P('shots', 'depth'), may hold values from -6 to 6
- fwd_snap: bfloat16 [32, 4, 128, 128, 128], P('shots', None, 'depth'), may hold values from -6 to 6
- velocity: float32 [128, 128, 128], P('depth', 'shots'), may hold values from 1 to 2
- density: float32 [128, 128, 128], P('depth', 'shots'), may hold values from 1 to 2
- shot_count: int32 [32], P('shots'), may hold values from 1 to 12, 128 in all
- rec_x: int32 [32, 256], P('shots'), may hold values from 0 to 127
- rec_y: int32 [32, 256], P('shots'), may hold values from 0 to 127
- residual: float32 [32, 4, 256], P('shots'), may hold values from -6 to 6
Outputs:
- out_now: float32 [32, 128, 128, 128], P('shots', 'depth')
- out_prev: float32 [32, 128, 128, 128], P('shots', 'depth')
- grad_vel: float32 [128, 128, 128], P('depth', 'shots')
The draws below stay inside these ranges and needn't reach their ends.
Inputs may be any that keep to these rules, and one draw needn't show every extreme that they name: `shot_count`: the counts sum to 128; the largest is exactly 12.
All inputs are finite; a program needn't handle non-finite values.
Results may differ from the reference program's by a relative error of at most 0.0003.
Values sent between devices are 32-bit elements; how exact they have to be, the bound alone decides.
No kernel may reach another device: no remote copies, remote signals or barrier semaphores. Data moves between devices by JAX's collectives and lax.ppermute only.
A program may use at most 64 MiB of HBM per device.

```python
import math
import jax
import jax.numpy as jnp
import numpy as np
from jax import lax

NX = 128
NY = 128
STEPS = 4
NREC = 256
GROUPS = 32
NZ = 128


def set_ends(array, own_key, smallest, top_value):
    shape = array.shape
    spot = [jax.random.randint(jax.random.fold_in(own_key, axis), (), 0, shape[axis]) for axis in range(len(shape))]
    array = array.at[tuple(spot)].set(smallest)
    longest = shape.index(max(shape))
    spot[longest] = (spot[longest] + 1) % shape[longest]
    return array.at[tuple(spot)].set(top_value)


def shard_levels(stream_key, shape, pieces, low, top_value):
    level = 1.0
    for axis_at, parts in pieces:
        draws = jax.random.uniform(jax.random.fold_in(jax.random.fold_in(stream_key, 6), axis_at), (parts,), jnp.float32, low / len(pieces), top_value / len(pieces))
        level = level * jnp.repeat(jnp.exp(draws), shape[axis_at] // parts).reshape((-1,) + (1,) * (len(shape) - 1 - axis_at))
    return level


def split_up(amount, total, bound, slope):
    portions = [(1 << 20) // math.isqrt(grade ** slope) + 1 for grade in range(2, amount + 1)]
    rest, holding = total - bound - (amount - 1), [1] * (amount - 1)
    while rest > 0:
        movable = [i for i in range(amount - 1) if holding[i] < bound]
        whole, left = sum([portions[i] for i in movable]), rest
        for i in movable:
            more = min(bound - holding[i], max(1, left * portions[i] // whole), rest)
            holding[i] = holding[i] + more
            rest = rest - more
    return np.array([bound] + holding)


def ragged(stream_key, number_of, total, reach, lean):
    if number_of == 2:
        one = jax.random.randint(stream_key, (), max(1, total - reach), min(reach, total - 1) + 1)
        return jnp.stack([one, total - one])
    sizes = jnp.asarray(split_up(number_of, total, reach, lean), jnp.int32)
    pairs = (number_of - 1) // 2
    source_of, taker = sizes[1:1 + 2 * pairs:2], sizes[2:2 + 2 * pairs:2]
    margin = jnp.minimum(source_of - 1, reach - taker)
    moved = jax.random.randint(jax.random.fold_in(stream_key, 1), (pairs,), 0, 1 << 20) % (margin + 1)
    sizes = sizes.at[1:1 + 2 * pairs:2].set(source_of - moved).at[2:2 + 2 * pairs:2].set(taker + moved)
    return sizes[jax.random.permutation(jax.random.fold_in(stream_key, 2), number_of)]


def centred(own_key, extent, deviation, bound, pieces=(), dtype=jnp.bfloat16):
    level = shard_levels(own_key, extent, pieces, -0.22, 0.18) if pieces else 1.0
    entries = jax.random.normal(own_key, extent, jnp.float32) * deviation * level
    return jnp.minimum(jnp.maximum(entries, -bound), bound).astype(dtype)


def setup_inputs(seed: int = 0) -> dict:
    key_list = jax.random.split(jax.random.key(seed), 10)
    return {
        "adj_now": centred(key_list[0], (GROUPS, NZ, NX, NY), 1.0, 6.0, ((0, 32), (1, 8)), jnp.float32),
        "adj_prev": centred(key_list[1], (GROUPS, NZ, NX, NY), 1.0, 6.0, ((0, 32), (1, 8)), jnp.float32),
        "fwd_snap": centred(key_list[2], (GROUPS, STEPS, NZ, NX, NY), 1.0, 6.0, ((0, 32), (2, 8))),
        "velocity": jnp.clip(jnp.exp(math.log(2.0) - 0.6931472 * jax.random.uniform(key_list[3], (NZ, NX, NY), jnp.float32) ** shard_levels(key_list[3], (NZ, NX, NY), ((0, 8), (1, 32)), -0.2, 0.2)), 1.0, 2.0),
        "density": jnp.clip(jnp.exp(math.log(2.0) - 0.6931472 * jax.random.uniform(key_list[4], (NZ, NX, NY), jnp.float32) ** shard_levels(key_list[4], (NZ, NX, NY), ((0, 8), (1, 32)), -0.2, 0.2)), 1.0, 2.0),
        "shot_count": ragged(key_list[5], GROUPS, 4 * GROUPS, 12, 2).astype(jnp.int32),
        "rec_x": set_ends(jax.random.randint(key_list[6], (GROUPS, NREC), 0, NX), jax.random.fold_in(key_list[6], 1), 0, NX - 1).astype(jnp.int32),
        "rec_y": set_ends(jax.random.randint(key_list[7], (GROUPS, NREC), 0, NY), jax.random.fold_in(key_list[7], 1), 0, NY - 1).astype(jnp.int32),
        "residual": centred(key_list[8], (GROUPS, STEPS, NREC), 1.0, 6.0, ((0, 32),), jnp.float32),
    }


def operate(field, buoy):
    padded = jnp.pad(field, 1)
    bpad = jnp.pad(buoy, 1)
    total = jnp.zeros_like(field)
    for axis in range(3):
        center = [slice(1, -1)] * 3
        ahead = list(center)
        behind = list(center)
        ahead[axis] = slice(2, None)
        behind[axis] = slice(0, -2)
        pc, pa, pb = padded[tuple(center)], padded[tuple(ahead)], padded[tuple(behind)]
        bc, ba, bb = bpad[tuple(center)], bpad[tuple(ahead)], bpad[tuple(behind)]
        total = total + 0.5 * (bc + ba) * (pa - pc) - 0.5 * (bb + bc) * (pc - pb)
    return total


def reference(adj_now, adj_prev, fwd_snap, velocity, density, shot_count, rec_x, rec_y, residual):
    kappa = density * velocity * velocity
    buoy = 1.0 / density

    def one_group(items):
        cur, old, snaps, count, rx, ry, res = items
        image = jnp.zeros_like(cur)
        for step in range(STEPS):
            t = STEPS - 1 - step
            plane = jnp.zeros((NX, NY), jnp.float32).at[rx, ry].add(res[t])
            source = jnp.zeros_like(cur).at[2].set(plane)
            new = 2.0 * cur - old + 0.08 * kappa * operate(cur, buoy) + 0.08 * source
            image = image + snaps[t].astype(jnp.float32) * new
            old = cur
            cur = new
        return cur, old, count.astype(jnp.float32) * image

    def scan_body(total, items):
        cur, old, weighted = one_group(items)
        return total + weighted, (cur, old)

    total, (out_now, out_prev) = lax.scan(scan_body, jnp.zeros((NZ, NX, NY), jnp.float32), (adj_now, adj_prev, fwd_snap, shot_count, rec_x, rec_y, residual))
    grad_vel = 2.0 * density * velocity * total / (4.0 * GROUPS)
    return out_now, out_prev, grad_vel
```

```python
import jax
import jax.numpy as jnp
from jax import lax
from jax.sharding import PartitionSpec as P


def with_halo(shard, sides, width):
    for axis, dim in sides:
        peers, length = (lax.axis_size(axis), shard.shape[dim])
        up = [(i, (i + 1) % peers) for i in range(peers - 1)]
        down = [(j, i) for i, j in up]
        last = lax.slice_in_dim(shard, length - width, length, axis=dim)
        first = lax.slice_in_dim(shard, 0, width, axis=dim)
        before = lax.ppermute(last, axis, up)
        after = lax.ppermute(first, axis, down)
        shard = jnp.concatenate([before, shard, after], axis=dim)
    return shard


def bit_order(peers):
    return list(range(peers.bit_length() - 1))


def gather_rows(shard, axis, dim):
    peers = lax.axis_size(axis)
    me = lax.axis_index(axis)
    pieces = jnp.expand_dims(shard, dim)
    for b in reversed(bit_order(peers)):
        pairs = [(i, i ^ (1 << b)) for i in range(peers)]
        got = lax.ppermute(pieces, axis, pairs)
        mine = (me >> b) & 1
        lo = jnp.where(mine == 0, pieces, got)
        hi = jnp.where(mine == 0, got, pieces)
        both = jnp.stack([lo, hi], axis=dim + 1)
        shape = list(pieces.shape)
        shape[dim] = shape[dim] * 2
        pieces = both.reshape(shape)
    shape = list(shard.shape)
    shape[dim] = shape[dim] * peers
    return pieces.reshape(shape)


def scatter_rows(full, axis, dim):
    peers = lax.axis_size(axis)
    me = lax.axis_index(axis)
    nbits = peers.bit_length() - 1
    rows = full.shape[dim] // peers
    shape = list(full.shape)
    blocks = full.reshape(shape[:dim] + [2] * nbits + [rows] + shape[dim + 1:])
    for b in bit_order(peers):
        where = dim + (nbits - 1 - b)
        mine = (me >> b) & 1
        keep = lax.dynamic_index_in_dim(blocks, mine, axis=where, keepdims=False)
        send = lax.dynamic_index_in_dim(blocks, 1 - mine, axis=where, keepdims=False)
        pairs = [(i, i ^ (1 << b)) for i in range(peers)]
        got = lax.ppermute(send, axis, pairs)
        blocks = keep + got
    return blocks


def operate(field, buoy):
    padded = jnp.pad(field, 1)
    bpad = jnp.pad(buoy, 1)
    total = jnp.zeros_like(field)
    for axis in range(3):
        center = [slice(1, -1)] * 3
        ahead = list(center)
        behind = list(center)
        ahead[axis] = slice(2, None)
        behind[axis] = slice(0, -2)
        pc, pa, pb = (padded[tuple(center)], padded[tuple(ahead)], padded[tuple(behind)])
        bc, ba, bb = (bpad[tuple(center)], bpad[tuple(ahead)], bpad[tuple(behind)])
        total = total + 0.5 * (bc + ba) * (pa - pc) - 0.5 * (bb + bc) * (pc - pb)
    return total


def source_plane(rows_x, rows_y, amounts, width_x, width_y):
    onehot_x = (rows_x[:, None] == jnp.arange(width_x, dtype=jnp.int32)[None, :]).astype(
        jnp.float32
    )
    onehot_y = (rows_y[:, None] == jnp.arange(width_y, dtype=jnp.int32)[None, :]).astype(
        jnp.float32
    )
    return jnp.dot((onehot_x * amounts[:, None]).T, onehot_y, precision=lax.Precision.HIGHEST)


def body(adj_now, adj_prev, fwd_snap, velocity, density, shot_count, rec_x, rec_y, residual):
    depth_planes = adj_now.shape[1]
    width_x = adj_now.shape[2]
    width_y = adj_now.shape[3]
    steps = fwd_snap.shape[1]
    groups = lax.axis_size("shots")
    width = 1
    local = jnp.stack([density * velocity * velocity, 1.0 / density])
    packed = gather_rows(local, "shots", 2)
    extended = with_halo(packed, (("depth", 1),), width)
    buoy_ext = extended[1]
    first = lax.axis_index("depth") * depth_planes
    snaps = fwd_snap[0]
    rows_x = rec_x[0]
    rows_y = rec_y[0]
    image = jnp.zeros((depth_planes, width_x, width_y), jnp.float32)
    kappa_ext = extended[0, width : width + depth_planes]
    global_plane = first + jnp.arange(depth_planes, dtype=jnp.int32)
    at_receivers = (global_plane == 2).astype(jnp.float32)[:, None, None]
    current = adj_now[0]
    older = adj_prev[0]
    for step in range(steps):
        moment = steps - 1 - step
        rimmed_field = with_halo(current[None], (("depth", 1),), 1)[0]
        plane = source_plane(rows_x, rows_y, residual[0, moment], width_x, width_y)
        spread = operate(rimmed_field, buoy_ext)[1:-1]
        newer = (
            2.0 * current - older + 0.08 * kappa_ext * spread + 0.08 * at_receivers * plane[None]
        )
        image = image + snaps[moment].astype(jnp.float32) * newer
        older = current
        current = newer
    weighted = shot_count[0].astype(jnp.float32) * image
    summed = scatter_rows(weighted, "shots", 1)
    grad_vel = 2.0 * density * velocity * summed / (4.0 * groups)
    return (current[None], older[None], grad_vel)


def solution(mesh):
    in_specs = (
        P("shots", "depth", None, None),
        P("shots", "depth", None, None),
        P("shots", None, "depth", None, None),
        P("depth", "shots", None),
        P("depth", "shots", None),
        P("shots"),
        P("shots", None),
        P("shots", None),
        P("shots", None, None),
    )
    out_specs = (
        P("shots", "depth", None, None),
        P("shots", "depth", None, None),
        P("depth", "shots", None),
    )
    return jax.shard_map(body, mesh=mesh, in_specs=in_specs, out_specs=out_specs, check_vma=False)
```

```python
import jax
import jax.numpy as jnp
from jax import lax
from jax.sharding import PartitionSpec as P
from jax.experimental import pallas as pl
from jax.experimental.pallas import tpu as pltpu

INTERPRET = False

HALO = 4


def shift_fwd(v, axis, n):
    r = pltpu.roll(v, n - 1, axis)
    idx = lax.broadcasted_iota(jnp.int32, v.shape, axis)
    return jnp.where(idx == n - 1, 0.0, r)


def shift_bwd(v, axis, n):
    r = pltpu.roll(v, 1, axis)
    idx = lax.broadcasted_iota(jnp.int32, v.shape, axis)
    return jnp.where(idx == 0, 0.0, r)


def term(bc, ba, bb, pc, pa, pb):
    return 0.5 * (bc + ba) * (pa - pc) - 0.5 * (bb + bc) * (pc - pb)


def stencil_kernel(count_ref, adj_ref, mat_ref, snap_ref, src_ref, now_ref, prev_ref, img_ref, pbuf, qbuf):
    ext = adj_ref.shape[1]
    nx, ny = adj_ref.shape[2], adj_ref.shape[3]
    steps = snap_ref.shape[0]
    count = count_ref[0]

    def one_step(step, cur, old, dst, lo, hi):
        moment = steps - 1 - step

        def plane(e, carry):
            pc = cur(e)
            pa = cur(e + 1)
            pb = cur(e - 1)
            bc = mat_ref[1, e]
            ba = mat_ref[1, e + 1]
            bb = mat_ref[1, e - 1]
            total = term(bc, ba, bb, pc, pa, pb)
            total = total + term(bc, shift_fwd(bc, 0, nx), shift_bwd(bc, 0, nx),
                                 pc, shift_fwd(pc, 0, nx), shift_bwd(pc, 0, nx))
            total = total + term(bc, shift_fwd(bc, 1, ny), shift_bwd(bc, 1, ny),
                                 pc, shift_fwd(pc, 1, ny), shift_bwd(pc, 1, ny))
            weight = jnp.where(e == HALO + 2, 1.0, 0.0)
            new = 2.0 * pc - old(e) + 0.08 * mat_ref[0, e] * total + 0.08 * src_ref[moment] * weight
            dst(e, new)
            inner = jnp.logical_and(e >= HALO, e < ext - HALO)

            @pl.when(inner)
            def _():
                z = e - HALO
                gained = snap_ref[moment, z].astype(jnp.float32) * new
                if step == 0:
                    img_ref[z] = gained
                elif step == steps - 1:
                    img_ref[z] = count * (img_ref[z] + gained)
                else:
                    img_ref[z] = img_ref[z] + gained
            return carry

        lax.fori_loop(lo, hi, plane, 0)

    def rd(ref, k=None):
        if k is None:
            return lambda e: ref[e]
        return lambda e: ref[k, e]

    def wr(ref):
        def f(e, v):
            ref[e] = v
        return f

    def wr_inner(ref, out):
        def f(e, v):
            ref[e] = v
            @pl.when(jnp.logical_and(e >= HALO, e < ext - HALO))
            def _():
                out[e - HALO] = v
        return f

    def wr_out(out):
        def f(e, v):
            out[e - HALO] = v
        return f

    one_step(0, rd(adj_ref, 0), rd(adj_ref, 1), wr(pbuf), 1, ext - 1)
    one_step(1, rd(pbuf), rd(adj_ref, 0), wr(qbuf), 2, ext - 2)
    one_step(2, rd(qbuf), rd(pbuf), wr_inner(pbuf, prev_ref), 3, ext - 3)
    one_step(3, rd(pbuf), rd(qbuf), wr_out(now_ref), HALO, ext - HALO)


def run_steps(count, adj_ext, mat_ext, snaps, src):
    ext, nx, ny = adj_ext.shape[1:]
    planes = ext - 2 * HALO
    vmem = pltpu.VMEM
    out_shape = [jax.ShapeDtypeStruct((planes, nx, ny), jnp.float32)] * 3
    return pl.pallas_call(
        stencil_kernel,
        out_shape=out_shape,
        in_specs=[pl.BlockSpec(memory_space=pltpu.SMEM)] + [pl.BlockSpec(memory_space=vmem)] * 4,
        out_specs=[pl.BlockSpec(memory_space=vmem)] * 3,
        scratch_shapes=[pltpu.VMEM((ext, nx, ny), jnp.float32)] * 2,
        compiler_params=pltpu.CompilerParams(vmem_limit_bytes=48 * 1024 * 1024),
        interpret=INTERPRET,
    )(count, adj_ext, mat_ext, snaps, src)


def with_halo(shard, sides, width):
    for axis, dim in sides:
        peers, length = (lax.axis_size(axis), shard.shape[dim])
        up = [(i, (i + 1) % peers) for i in range(peers - 1)]
        down = [(j, i) for i, j in up]
        last = lax.slice_in_dim(shard, length - width, length, axis=dim)
        first = lax.slice_in_dim(shard, 0, width, axis=dim)
        before = lax.ppermute(last, axis, up)
        after = lax.ppermute(first, axis, down)
        shard = jnp.concatenate([before, shard, after], axis=dim)
    return shard


def bit_order(peers):
    return list(range(peers.bit_length() - 1))


def gather_rows(shard, axis, dim):
    peers = lax.axis_size(axis)
    me = lax.axis_index(axis)
    pieces = jnp.expand_dims(shard, dim)
    for b in reversed(bit_order(peers)):
        pairs = [(i, i ^ (1 << b)) for i in range(peers)]
        got = lax.ppermute(pieces, axis, pairs)
        mine = (me >> b) & 1
        lo = jnp.where(mine == 0, pieces, got)
        hi = jnp.where(mine == 0, got, pieces)
        both = jnp.stack([lo, hi], axis=dim + 1)
        shape = list(pieces.shape)
        shape[dim] = shape[dim] * 2
        pieces = both.reshape(shape)
    shape = list(shard.shape)
    shape[dim] = shape[dim] * peers
    return pieces.reshape(shape)


def scatter_rows(full, axis, dim):
    peers = lax.axis_size(axis)
    me = lax.axis_index(axis)
    nbits = peers.bit_length() - 1
    rows = full.shape[dim] // peers
    shape = list(full.shape)
    blocks = full.reshape(shape[:dim] + [2] * nbits + [rows] + shape[dim + 1:])
    for b in bit_order(peers):
        where = dim + (nbits - 1 - b)
        mine = (me >> b) & 1
        keep = lax.dynamic_index_in_dim(blocks, mine, axis=where, keepdims=False)
        send = lax.dynamic_index_in_dim(blocks, 1 - mine, axis=where, keepdims=False)
        pairs = [(i, i ^ (1 << b)) for i in range(peers)]
        got = lax.ppermute(send, axis, pairs)
        blocks = keep + got
    return blocks


def operate(field, buoy):
    padded = jnp.pad(field, 1)
    bpad = jnp.pad(buoy, 1)
    total = jnp.zeros_like(field)
    for axis in range(3):
        center = [slice(1, -1)] * 3
        ahead = list(center)
        behind = list(center)
        ahead[axis] = slice(2, None)
        behind[axis] = slice(0, -2)
        pc, pa, pb = (padded[tuple(center)], padded[tuple(ahead)], padded[tuple(behind)])
        bc, ba, bb = (bpad[tuple(center)], bpad[tuple(ahead)], bpad[tuple(behind)])
        total = total + 0.5 * (bc + ba) * (pa - pc) - 0.5 * (bb + bc) * (pc - pb)
    return total


def source_plane(rows_x, rows_y, amounts, width_x, width_y):
    onehot_x = (rows_x[:, None] == jnp.arange(width_x, dtype=jnp.int32)[None, :]).astype(
        jnp.float32
    )
    onehot_y = (rows_y[:, None] == jnp.arange(width_y, dtype=jnp.int32)[None, :]).astype(
        jnp.float32
    )
    return jnp.dot((onehot_x * amounts[:, None]).T, onehot_y, precision=lax.Precision.HIGHEST)


def body(adj_now, adj_prev, fwd_snap, velocity, density, shot_count, rec_x, rec_y, residual):
    width_x = adj_now.shape[2]
    width_y = adj_now.shape[3]
    steps = fwd_snap.shape[1]
    groups = lax.axis_size("shots")
    local = jnp.stack([density * velocity * velocity, 1.0 / density])
    packed = gather_rows(local, "shots", 2)
    mat_ext = with_halo(packed, (("depth", 1),), HALO)
    adj_ext = with_halo(jnp.stack([adj_now[0], adj_prev[0]]), (("depth", 1),), HALO)
    holds_source = (lax.axis_index("depth") == 0).astype(jnp.float32)
    src = jnp.stack(
        [source_plane(rec_x[0], rec_y[0], residual[0, t], width_x, width_y) for t in range(steps)]
    ) * holds_source
    count = shot_count.astype(jnp.float32)
    current, older, weighted = run_steps(count, adj_ext, mat_ext, fwd_snap[0], src)
    summed = scatter_rows(weighted, "shots", 1)
    grad_vel = 2.0 * density * velocity * summed / (4.0 * groups)
    return (current[None], older[None], grad_vel)


def solution(mesh):
    in_specs = (
        P("shots", "depth", None, None),
        P("shots", "depth", None, None),
        P("shots", None, "depth", None, None),
        P("depth", "shots", None),
        P("depth", "shots", None),
        P("shots"),
        P("shots", None),
        P("shots", None),
        P("shots", None, None),
    )
    out_specs = (
        P("shots", "depth", None, None),
        P("shots", "depth", None, None),
        P("depth", "shots", None),
    )
    return jax.shard_map(body, mesh=mesh, in_specs=in_specs, out_specs=out_specs, check_vma=False)
```

```python
import jax
import jax.numpy as jnp
from jax import lax
from jax.sharding import PartitionSpec as P
from jax.experimental import pallas as pl
from jax.experimental.pallas import tpu as pltpu

INTERPRET = False

HALO = 4


def shift_fwd(v, axis, n):
    r = pltpu.roll(v, n - 1, axis)
    idx = lax.broadcasted_iota(jnp.int32, v.shape, axis)
    return jnp.where(idx == n - 1, 0.0, r)


def shift_bwd(v, axis):
    r = pltpu.roll(v, 1, axis)
    idx = lax.broadcasted_iota(jnp.int32, v.shape, axis)
    return jnp.where(idx == 0, 0.0, r)


def stencil_kernel(count_ref, adj_ref, mat_ref, snap_ref, src_ref, now_ref, prev_ref, img_ref,
                   pbuf, qbuf, kz, kxf, kxb, kyf, kyb, kk):
    ext = adj_ref.shape[1]
    nx, ny = adj_ref.shape[2], adj_ref.shape[3]
    steps = snap_ref.shape[0]
    count = count_ref[0]

    def weights(e, carry):
        bc = mat_ref[1, e]
        kz[e] = 0.5 * (bc + mat_ref[1, e + 1])
        kxf[e] = 0.5 * (bc + shift_fwd(bc, 0, nx))
        kxb[e] = 0.5 * (shift_bwd(bc, 0) + bc)
        kyf[e] = 0.5 * (bc + shift_fwd(bc, 1, ny))
        kyb[e] = 0.5 * (shift_bwd(bc, 1) + bc)
        kk[e] = 0.08 * mat_ref[0, e]
        return carry

    lax.fori_loop(0, ext - 1, weights, 0)

    def one_step(step, cur, old, dst, lo, hi):
        moment = steps - 1 - step

        def plane(e, carry):
            pc = cur(e)
            total = kz[e] * (cur(e + 1) - pc) - kz[e - 1] * (pc - cur(e - 1))
            total = total + (kxf[e] * (shift_fwd(pc, 0, nx) - pc) - kxb[e] * (pc - shift_bwd(pc, 0)))
            total = total + (kyf[e] * (shift_fwd(pc, 1, ny) - pc) - kyb[e] * (pc - shift_bwd(pc, 1)))
            weight = jnp.where(e == HALO + 2, 1.0, 0.0)
            new = 2.0 * pc - old(e) + kk[e] * total + 0.08 * src_ref[moment] * weight
            dst(e, new)
            inner = jnp.logical_and(e >= HALO, e < ext - HALO)

            @pl.when(inner)
            def _():
                z = e - HALO
                gained = snap_ref[moment, z].astype(jnp.float32) * new
                if step == 0:
                    img_ref[z] = gained
                elif step == steps - 1:
                    img_ref[z] = count * (img_ref[z] + gained)
                else:
                    img_ref[z] = img_ref[z] + gained

            return carry

        lax.fori_loop(lo, hi, plane, 0)

    def rd(ref, k=None):
        if k is None:
            return lambda e: ref[e]
        return lambda e: ref[k, e]

    def wr(ref):
        def f(e, v):
            ref[e] = v

        return f

    def wr_inner(ref, out):
        def f(e, v):
            ref[e] = v

            @pl.when(jnp.logical_and(e >= HALO, e < ext - HALO))
            def _():
                out[e - HALO] = v

        return f

    def wr_out(out):
        def f(e, v):
            out[e - HALO] = v

        return f

    one_step(0, rd(adj_ref, 0), rd(adj_ref, 1), wr(pbuf), 1, ext - 1)
    one_step(1, rd(pbuf), rd(adj_ref, 0), wr(qbuf), 2, ext - 2)
    one_step(2, rd(qbuf), rd(pbuf), wr_inner(pbuf, prev_ref), 3, ext - 3)
    one_step(3, rd(pbuf), rd(qbuf), wr_out(now_ref), HALO, ext - HALO)


def run_steps(count, adj_ext, mat_ext, snaps, src):
    ext, nx, ny = adj_ext.shape[1:]
    planes = ext - 2 * HALO
    vmem = pltpu.VMEM
    out_shape = [jax.ShapeDtypeStruct((planes, nx, ny), jnp.float32)] * 3
    return pl.pallas_call(
        stencil_kernel,
        out_shape=out_shape,
        in_specs=[pl.BlockSpec(memory_space=pltpu.SMEM)] + [pl.BlockSpec(memory_space=vmem)] * 4,
        out_specs=[pl.BlockSpec(memory_space=vmem)] * 3,
        scratch_shapes=[pltpu.VMEM((ext, nx, ny), jnp.float32)] * 8,
        compiler_params=pltpu.CompilerParams(vmem_limit_bytes=48 * 1024 * 1024),
        interpret=INTERPRET,
    )(count, adj_ext, mat_ext, snaps, src)


def with_halo(shard, sides, width):
    for axis, dim in sides:
        peers, length = (lax.axis_size(axis), shard.shape[dim])
        up = [(i, (i + 1) % peers) for i in range(peers - 1)]
        down = [(j, i) for i, j in up]
        last = lax.slice_in_dim(shard, length - width, length, axis=dim)
        first = lax.slice_in_dim(shard, 0, width, axis=dim)
        before = lax.ppermute(last, axis, up)
        after = lax.ppermute(first, axis, down)
        shard = jnp.concatenate([before, shard, after], axis=dim)
    return shard


def bit_order(peers):
    return list(range(peers.bit_length() - 1))


def gather_rows(shard, axis, dim):
    peers = lax.axis_size(axis)
    me = lax.axis_index(axis)
    pieces = jnp.expand_dims(shard, dim)
    for b in reversed(bit_order(peers)):
        pairs = [(i, i ^ (1 << b)) for i in range(peers)]
        got = lax.ppermute(pieces, axis, pairs)
        mine = (me >> b) & 1
        lo = jnp.where(mine == 0, pieces, got)
        hi = jnp.where(mine == 0, got, pieces)
        both = jnp.stack([lo, hi], axis=dim + 1)
        shape = list(pieces.shape)
        shape[dim] = shape[dim] * 2
        pieces = both.reshape(shape)
    shape = list(shard.shape)
    shape[dim] = shape[dim] * peers
    return pieces.reshape(shape)


def scatter_rows(full, axis, dim):
    peers = lax.axis_size(axis)
    me = lax.axis_index(axis)
    nbits = peers.bit_length() - 1
    rows = full.shape[dim] // peers
    shape = list(full.shape)
    blocks = full.reshape(shape[:dim] + [2] * nbits + [rows] + shape[dim + 1:])
    for b in bit_order(peers):
        where = dim + (nbits - 1 - b)
        mine = (me >> b) & 1
        keep = lax.dynamic_index_in_dim(blocks, mine, axis=where, keepdims=False)
        send = lax.dynamic_index_in_dim(blocks, 1 - mine, axis=where, keepdims=False)
        pairs = [(i, i ^ (1 << b)) for i in range(peers)]
        got = lax.ppermute(send, axis, pairs)
        blocks = keep + got
    return blocks


def source_plane(rows_x, rows_y, amounts, width_x, width_y):
    onehot_x = (rows_x[:, None] == jnp.arange(width_x, dtype=jnp.int32)[None, :]).astype(
        jnp.float32
    )
    onehot_y = (rows_y[:, None] == jnp.arange(width_y, dtype=jnp.int32)[None, :]).astype(
        jnp.float32
    )
    return jnp.dot((onehot_x * amounts[:, None]).T, onehot_y, precision=lax.Precision.HIGHEST)


def body(adj_now, adj_prev, fwd_snap, velocity, density, shot_count, rec_x, rec_y, residual):
    width_x = adj_now.shape[2]
    width_y = adj_now.shape[3]
    steps = fwd_snap.shape[1]
    groups = lax.axis_size("shots")
    adj_ext = with_halo(jnp.stack([adj_now[0], adj_prev[0]]), (("depth", 1),), HALO)
    local = jnp.stack([density * velocity * velocity, 1.0 / density])
    local_ext = with_halo(local, (("depth", 1),), HALO)
    mat_ext = gather_rows(local_ext, "shots", 2)
    holds_source = (lax.axis_index("depth") == 0).astype(jnp.float32)
    src = jnp.stack(
        [source_plane(rec_x[0], rec_y[0], residual[0, t], width_x, width_y) for t in range(steps)]
    ) * holds_source
    count = shot_count.astype(jnp.float32)
    current, older, weighted = run_steps(count, adj_ext, mat_ext, fwd_snap[0], src)
    summed = scatter_rows(weighted, "shots", 1)
    grad_vel = 2.0 * density * velocity * summed / (4.0 * groups)
    return (current[None], older[None], grad_vel)


def solution(mesh):
    in_specs = (
        P("shots", "depth", None, None),
        P("shots", "depth", None, None),
        P("shots", None, "depth", None, None),
        P("depth", "shots", None),
        P("depth", "shots", None),
        P("shots"),
        P("shots", None),
        P("shots", None),
        P("shots", None, None),
    )
    out_specs = (
        P("shots", "depth", None, None),
        P("shots", "depth", None, None),
        P("depth", "shots", None),
    )
    return jax.shard_map(body, mesh=mesh, in_specs=in_specs, out_specs=out_specs, check_vma=False)
```

```python
import jax
import jax.numpy as jnp
from jax import lax
from jax.sharding import PartitionSpec as P
from jax.experimental import pallas as pl
from jax.experimental.pallas import tpu as pltpu

INTERPRET = False

HALO = 4


def shift_fwd(v, axis, n):
    r = pltpu.roll(v, n - 1, axis)
    idx = lax.broadcasted_iota(jnp.int32, v.shape, axis)
    return jnp.where(idx == n - 1, 0.0, r)


def shift_bwd(v, axis):
    r = pltpu.roll(v, 1, axis)
    idx = lax.broadcasted_iota(jnp.int32, v.shape, axis)
    return jnp.where(idx == 0, 0.0, r)


def stencil_kernel(count_ref, adj_ref, mat_ref, snap_ref, src_ref, now_ref, prev_ref, img_ref,
                   pbuf, qbuf, kz, kxf, kxb, kyf, kyb, kk):
    ext = adj_ref.shape[1]
    nx, ny = adj_ref.shape[2], adj_ref.shape[3]
    steps = snap_ref.shape[0]
    count = count_ref[0]

    def weights(e, carry):
        bc = mat_ref[1, e]
        kz[e] = 0.5 * (bc + mat_ref[1, e + 1])
        kxf[e] = 0.5 * (bc + shift_fwd(bc, 0, nx))
        kxb[e] = 0.5 * (shift_bwd(bc, 0) + bc)
        kyf[e] = 0.5 * (bc + shift_fwd(bc, 1, ny))
        kyb[e] = 0.5 * (shift_bwd(bc, 1) + bc)
        kk[e] = 0.08 * mat_ref[0, e]
        return carry

    lax.fori_loop(0, ext - 1, weights, 0)

    def one_step(step, cur, old, dst, lo, hi):
        moment = steps - 1 - step

        def plane(e, carry):
            pc = cur(e)
            total = kz[e] * (cur(e + 1) - pc) - kz[e - 1] * (pc - cur(e - 1))
            total = total + (kxf[e] * (shift_fwd(pc, 0, nx) - pc) - kxb[e] * (pc - shift_bwd(pc, 0)))
            total = total + (kyf[e] * (shift_fwd(pc, 1, ny) - pc) - kyb[e] * (pc - shift_bwd(pc, 1)))
            weight = jnp.where(e == HALO + 2, 1.0, 0.0)
            new = 2.0 * pc - old(e) + kk[e] * total + 0.08 * src_ref[moment] * weight
            dst(e, new)
            inner = jnp.logical_and(e >= HALO, e < ext - HALO)

            @pl.when(inner)
            def _():
                z = e - HALO
                gained = snap_ref[moment, z].astype(jnp.float32) * new
                if step == 0:
                    img_ref[z] = gained
                elif step == steps - 1:
                    img_ref[z] = count * (img_ref[z] + gained)
                else:
                    img_ref[z] = img_ref[z] + gained

            return carry

        lax.fori_loop(lo, hi, plane, 0)

    def rd(ref, k=None):
        if k is None:
            return lambda e: ref[e]
        return lambda e: ref[k, e]

    def wr(ref):
        def f(e, v):
            ref[e] = v

        return f

    def wr_inner(ref, out):
        def f(e, v):
            ref[e] = v

            @pl.when(jnp.logical_and(e >= HALO, e < ext - HALO))
            def _():
                out[e - HALO] = v

        return f

    def wr_out(out):
        def f(e, v):
            out[e - HALO] = v

        return f

    one_step(0, rd(adj_ref, 0), rd(adj_ref, 1), wr(pbuf), 1, ext - 1)
    one_step(1, rd(pbuf), rd(adj_ref, 0), wr(qbuf), 2, ext - 2)
    one_step(2, rd(qbuf), rd(pbuf), wr_inner(pbuf, prev_ref), 3, ext - 3)
    one_step(3, rd(pbuf), rd(qbuf), wr_out(now_ref), HALO, ext - HALO)


def run_steps(count, adj_ext, mat_ext, snaps, src):
    ext, nx, ny = adj_ext.shape[1:]
    planes = ext - 2 * HALO
    vmem = pltpu.VMEM
    out_shape = [jax.ShapeDtypeStruct((planes, nx, ny), jnp.float32)] * 3
    return pl.pallas_call(
        stencil_kernel,
        out_shape=out_shape,
        in_specs=[pl.BlockSpec(memory_space=pltpu.SMEM)] + [pl.BlockSpec(memory_space=vmem)] * 4,
        out_specs=[pl.BlockSpec(memory_space=vmem)] * 3,
        scratch_shapes=[pltpu.VMEM((ext, nx, ny), jnp.float32)] * 8,
        compiler_params=pltpu.CompilerParams(vmem_limit_bytes=48 * 1024 * 1024),
        interpret=INTERPRET,
    )(count, adj_ext, mat_ext, snaps, src)


def with_halo(shard, sides, width):
    for axis, dim in sides:
        peers, length = (lax.axis_size(axis), shard.shape[dim])
        up = [(i, (i + 1) % peers) for i in range(peers - 1)]
        down = [(j, i) for i, j in up]
        last = lax.slice_in_dim(shard, length - width, length, axis=dim)
        first = lax.slice_in_dim(shard, 0, width, axis=dim)
        before = lax.ppermute(last, axis, up)
        after = lax.ppermute(first, axis, down)
        shard = jnp.concatenate([before, shard, after], axis=dim)
    return shard


def gather_rows(shard, axis, dim, direct):
    peers = lax.axis_size(axis)
    me = lax.axis_index(axis)
    nbits = peers.bit_length() - 1
    low = nbits - direct
    span, stride = 1 << direct, 1 << low
    top = me >> low
    got = [shard]
    for k in range(1, span):
        pairs = [(i, (((i >> low) + k) % span) * stride + (i % stride)) for i in range(peers)]
        got.append(lax.ppermute(shard, axis, pairs))
    ahead = jnp.stack([got[0]] + got[1:][::-1], axis=dim)
    pieces = jnp.roll(ahead, top, axis=dim)
    for b in reversed(range(low)):
        pairs = [(i, i ^ (1 << b)) for i in range(peers)]
        got = lax.ppermute(pieces, axis, pairs)
        mine = (me >> b) & 1
        lo = jnp.where(mine == 0, pieces, got)
        hi = jnp.where(mine == 0, got, pieces)
        both = jnp.stack([lo, hi], axis=dim + 1)
        shape = list(pieces.shape)
        shape[dim] = shape[dim] * 2
        pieces = both.reshape(shape)
    shape = list(shard.shape)
    shape[dim] = shape[dim] * peers
    return pieces.reshape(shape)


def scatter_rows(full, axis, dim, direct):
    peers = lax.axis_size(axis)
    me = lax.axis_index(axis)
    nbits = peers.bit_length() - 1
    low = nbits - direct
    span, stride = 1 << direct, 1 << low
    top = me >> low
    rows = full.shape[dim] // peers
    shape = list(full.shape)
    blocks = full.reshape(shape[:dim] + [span] + [2] * low + [rows] + shape[dim + 1:])
    for b in range(low):
        where = dim + 1 + (low - 1 - b)
        mine = (me >> b) & 1
        keep = lax.dynamic_index_in_dim(blocks, mine, axis=where, keepdims=False)
        send = lax.dynamic_index_in_dim(blocks, 1 - mine, axis=where, keepdims=False)
        pairs = [(i, i ^ (1 << b)) for i in range(peers)]
        got = lax.ppermute(send, axis, pairs)
        blocks = keep + got
    total = lax.dynamic_index_in_dim(blocks, top, axis=dim, keepdims=False)
    for k in range(1, span):
        pairs = [(i, (((i >> low) + k) % span) * stride + (i % stride)) for i in range(peers)]
        send = lax.dynamic_index_in_dim(blocks, (top + k) % span, axis=dim, keepdims=False)
        total = total + lax.ppermute(send, axis, pairs)
    return total


def source_plane(rows_x, rows_y, amounts, width_x, width_y):
    onehot_x = (rows_x[:, None] == jnp.arange(width_x, dtype=jnp.int32)[None, :]).astype(
        jnp.float32
    )
    onehot_y = (rows_y[:, None] == jnp.arange(width_y, dtype=jnp.int32)[None, :]).astype(
        jnp.float32
    )
    return jnp.dot((onehot_x * amounts[:, None]).T, onehot_y, precision=lax.Precision.HIGHEST)


def body(adj_now, adj_prev, fwd_snap, velocity, density, shot_count, rec_x, rec_y, residual):
    width_x = adj_now.shape[2]
    width_y = adj_now.shape[3]
    steps = fwd_snap.shape[1]
    groups = lax.axis_size("shots")
    adj_ext = with_halo(jnp.stack([adj_now[0], adj_prev[0]]), (("depth", 1),), HALO)
    local = jnp.stack([density * velocity * velocity, 1.0 / density])
    packed = gather_rows(local, "shots", 2, 3)
    mat_ext = with_halo(packed, (("depth", 1),), HALO)
    holds_source = (lax.axis_index("depth") == 0).astype(jnp.float32)
    src = jnp.stack(
        [source_plane(rec_x[0], rec_y[0], residual[0, t], width_x, width_y) for t in range(steps)]
    ) * holds_source
    count = shot_count.astype(jnp.float32)
    current, older, weighted = run_steps(count, adj_ext, mat_ext, fwd_snap[0], src)
    summed = scatter_rows(weighted, "shots", 1, 3)
    grad_vel = 2.0 * density * velocity * summed / (4.0 * groups)
    return (current[None], older[None], grad_vel)


def solution(mesh):
    in_specs = (
        P("shots", "depth", None, None),
        P("shots", "depth", None, None),
        P("shots", None, "depth", None, None),
        P("depth", "shots", None),
        P("depth", "shots", None),
        P("shots"),
        P("shots", None),
        P("shots", None),
        P("shots", None, None),
    )
    out_specs = (
        P("shots", "depth", None, None),
        P("shots", "depth", None, None),
        P("depth", "shots", None),
    )
    return jax.shard_map(body, mesh=mesh, in_specs=in_specs, out_specs=out_specs, check_vma=False)
```

```python
import jax
import jax.numpy as jnp
from jax import lax
from jax.sharding import PartitionSpec as P
from jax.experimental import pallas as pl
from jax.experimental.pallas import tpu as pltpu

INTERPRET = False

HALO = 4


def shift_fwd(v, axis, n):
    r = pltpu.roll(v, n - 1, axis)
    idx = lax.broadcasted_iota(jnp.int32, v.shape, axis)
    return jnp.where(idx == n - 1, 0.0, r)


def shift_bwd(v, axis):
    r = pltpu.roll(v, 1, axis)
    idx = lax.broadcasted_iota(jnp.int32, v.shape, axis)
    return jnp.where(idx == 0, 0.0, r)


def stencil_kernel(count_ref, now_hbm, prev_hbm, adj_lo, adj_hi, mat_hbm, mat_lo, mat_hi, snap_hbm,
                   src_hbm, now_ref, prev_ref, img_ref, curb, oldb, matb, snapb, srcb, pbuf, qbuf,
                   kz, kxf, kxb, kyf, kyb, kk, sems):
    ext = curb.shape[0]
    nx, ny = curb.shape[1], curb.shape[2]
    planes = ext - 2 * HALO
    steps = snapb.shape[0]
    count = count_ref[0]
    copies = []

    def fetch(src, dst):
        c = pltpu.make_async_copy(src, dst, sems.at[len(copies)])
        c.start()
        copies.append(c)
        return c

    inner_at, lo_at, hi_at = pl.ds(HALO, planes), pl.ds(0, HALO), pl.ds(HALO + planes, HALO)
    need_mat = [fetch(mat_hbm, matb.at[:, inner_at]), fetch(mat_lo, matb.at[:, lo_at]),
                fetch(mat_hi, matb.at[:, hi_at])]
    need_adj = [fetch(now_hbm, curb.at[inner_at]), fetch(adj_lo.at[0], curb.at[lo_at]),
                fetch(adj_hi.at[0], curb.at[hi_at]), fetch(prev_hbm, oldb.at[inner_at]),
                fetch(adj_lo.at[1], oldb.at[lo_at]), fetch(adj_hi.at[1], oldb.at[hi_at]),
                fetch(src_hbm, srcb)]
    need_snap = [fetch(snap_hbm.at[steps - 1 - step], snapb.at[steps - 1 - step])
                 for step in range(steps)]
    for c in need_mat:
        c.wait()

    def weights(e, carry):
        bc = matb[1, e]
        kz[e] = 0.5 * (bc + matb[1, e + 1])
        kxf[e] = 0.5 * (bc + shift_fwd(bc, 0, nx))
        kxb[e] = 0.5 * (shift_bwd(bc, 0) + bc)
        kyf[e] = 0.5 * (bc + shift_fwd(bc, 1, ny))
        kyb[e] = 0.5 * (shift_bwd(bc, 1) + bc)
        kk[e] = 0.08 * matb[0, e]
        return carry

    lax.fori_loop(0, ext - 1, weights, 0)
    for c in need_adj:
        c.wait()

    def one_step(step, cur, old, dst, lo, hi):
        moment = steps - 1 - step
        need_snap[step].wait()

        def plane(e, carry):
            pc = cur(e)
            total = kz[e] * (cur(e + 1) - pc) - kz[e - 1] * (pc - cur(e - 1))
            total = total + (kxf[e] * (shift_fwd(pc, 0, nx) - pc) - kxb[e] * (pc - shift_bwd(pc, 0)))
            total = total + (kyf[e] * (shift_fwd(pc, 1, ny) - pc) - kyb[e] * (pc - shift_bwd(pc, 1)))
            weight = jnp.where(e == HALO + 2, 1.0, 0.0)
            new = 2.0 * pc - old(e) + kk[e] * total + 0.08 * srcb[moment] * weight
            dst(e, new)
            inner = jnp.logical_and(e >= HALO, e < ext - HALO)

            @pl.when(inner)
            def _():
                z = e - HALO
                gained = snapb[moment, z].astype(jnp.float32) * new
                if step == 0:
                    img_ref[z] = gained
                elif step == steps - 1:
                    img_ref[z] = count * (img_ref[z] + gained)
                else:
                    img_ref[z] = img_ref[z] + gained

            return carry

        lax.fori_loop(lo, hi, plane, 0)

    def rd(ref):
        return lambda e: ref[e]

    def wr(ref):
        def f(e, v):
            ref[e] = v

        return f

    def wr_inner(ref, out):
        def f(e, v):
            ref[e] = v

            @pl.when(jnp.logical_and(e >= HALO, e < ext - HALO))
            def _():
                out[e - HALO] = v

        return f

    def wr_out(out):
        def f(e, v):
            out[e - HALO] = v

        return f

    one_step(0, rd(curb), rd(oldb), wr(pbuf), 1, ext - 1)
    one_step(1, rd(pbuf), rd(curb), wr(qbuf), 2, ext - 2)
    one_step(2, rd(qbuf), rd(pbuf), wr_inner(pbuf, prev_ref), 3, ext - 3)
    one_step(3, rd(pbuf), rd(qbuf), wr_out(now_ref), HALO, ext - HALO)


def run_steps(count, adj_now, adj_prev, adj_lo, adj_hi, mat, mat_lo, mat_hi, snaps, src):
    planes, nx, ny = adj_now.shape
    ext = planes + 2 * HALO
    steps = snaps.shape[0]
    vmem = pltpu.VMEM
    out_shape = [jax.ShapeDtypeStruct((planes, nx, ny), jnp.float32)] * 3
    field = pltpu.VMEM((ext, nx, ny), jnp.float32)
    return pl.pallas_call(
        stencil_kernel,
        out_shape=out_shape,
        in_specs=[pl.BlockSpec(memory_space=pltpu.SMEM)] + [pl.BlockSpec(memory_space=pl.ANY)] * 9,
        out_specs=[pl.BlockSpec(memory_space=vmem)] * 3,
        scratch_shapes=[field, field, pltpu.VMEM((2, ext, nx, ny), jnp.float32),
                        pltpu.VMEM(snaps.shape, snaps.dtype), pltpu.VMEM(src.shape, jnp.float32)]
        + [field] * 8 + [pltpu.SemaphoreType.DMA((10 + steps,))],
        compiler_params=pltpu.CompilerParams(vmem_limit_bytes=56 * 1024 * 1024),
        interpret=INTERPRET,
    )(count, adj_now, adj_prev, adj_lo, adj_hi, mat, mat_lo, mat_hi, snaps, src)


def halo_of(shard, axis, dim, width):
    peers, length = (lax.axis_size(axis), shard.shape[dim])
    up = [(i, (i + 1) % peers) for i in range(peers - 1)]
    down = [(j, i) for i, j in up]
    last = lax.slice_in_dim(shard, length - width, length, axis=dim)
    first = lax.slice_in_dim(shard, 0, width, axis=dim)
    return lax.ppermute(last, axis, up), lax.ppermute(first, axis, down)


def bit_order(peers):
    return list(range(peers.bit_length() - 1))


def gather_rows(shard, axis, dim):
    peers = lax.axis_size(axis)
    me = lax.axis_index(axis)
    pieces = jnp.expand_dims(shard, dim)
    for b in reversed(bit_order(peers)):
        pairs = [(i, i ^ (1 << b)) for i in range(peers)]
        got = lax.ppermute(pieces, axis, pairs)
        mine = (me >> b) & 1
        lo = jnp.where(mine == 0, pieces, got)
        hi = jnp.where(mine == 0, got, pieces)
        both = jnp.stack([lo, hi], axis=dim + 1)
        shape = list(pieces.shape)
        shape[dim] = shape[dim] * 2
        pieces = both.reshape(shape)
    shape = list(shard.shape)
    shape[dim] = shape[dim] * peers
    return pieces.reshape(shape)


def scatter_rows(full, axis, dim):
    peers = lax.axis_size(axis)
    me = lax.axis_index(axis)
    nbits = peers.bit_length() - 1
    rows = full.shape[dim] // peers
    shape = list(full.shape)
    blocks = full.reshape(shape[:dim] + [2] * nbits + [rows] + shape[dim + 1:])
    for b in bit_order(peers):
        where = dim + (nbits - 1 - b)
        mine = (me >> b) & 1
        keep = lax.dynamic_index_in_dim(blocks, mine, axis=where, keepdims=False)
        send = lax.dynamic_index_in_dim(blocks, 1 - mine, axis=where, keepdims=False)
        pairs = [(i, i ^ (1 << b)) for i in range(peers)]
        got = lax.ppermute(send, axis, pairs)
        blocks = keep + got
    return blocks


def source_plane(rows_x, rows_y, amounts, width_x, width_y):
    onehot_x = (rows_x[:, None] == jnp.arange(width_x, dtype=jnp.int32)[None, :]).astype(
        jnp.float32
    )
    onehot_y = (rows_y[:, None] == jnp.arange(width_y, dtype=jnp.int32)[None, :]).astype(
        jnp.float32
    )
    return jnp.dot((onehot_x * amounts[:, None]).T, onehot_y, precision=lax.Precision.HIGHEST)


def body(adj_now, adj_prev, fwd_snap, velocity, density, shot_count, rec_x, rec_y, residual):
    width_x = adj_now.shape[2]
    width_y = adj_now.shape[3]
    steps = fwd_snap.shape[1]
    groups = lax.axis_size("shots")
    adj_lo, adj_hi = halo_of(jnp.stack([adj_now[0], adj_prev[0]]), "depth", 1, HALO)
    local = jnp.stack([density * velocity * velocity, 1.0 / density])
    packed = gather_rows(local, "shots", 2)
    mat_lo, mat_hi = halo_of(packed, "depth", 1, HALO)
    holds_source = (lax.axis_index("depth") == 0).astype(jnp.float32)
    src = jnp.stack(
        [source_plane(rec_x[0], rec_y[0], residual[0, t], width_x, width_y) for t in range(steps)]
    ) * holds_source
    count = shot_count.astype(jnp.float32)
    current, older, weighted = run_steps(
        count, adj_now[0], adj_prev[0], adj_lo, adj_hi, packed, mat_lo, mat_hi, fwd_snap[0], src
    )
    summed = scatter_rows(weighted, "shots", 1)
    grad_vel = 2.0 * density * velocity * summed / (4.0 * groups)
    return (current[None], older[None], grad_vel)


def solution(mesh):
    in_specs = (
        P("shots", "depth", None, None),
        P("shots", "depth", None, None),
        P("shots", None, "depth", None, None),
        P("depth", "shots", None),
        P("depth", "shots", None),
        P("shots"),
        P("shots", None),
        P("shots", None),
        P("shots", None, None),
    )
    out_specs = (
        P("shots", "depth", None, None),
        P("shots", "depth", None, None),
        P("depth", "shots", None),
    )
    return jax.shard_map(body, mesh=mesh, in_specs=in_specs, out_specs=out_specs, check_vma=False)
```

```python
import jax
import jax.numpy as jnp
from jax import lax
from jax.sharding import PartitionSpec as P
from jax.experimental import pallas as pl
from jax.experimental.pallas import tpu as pltpu

INTERPRET = False

HALO = 4


def shift_fwd(v, axis, n):
    r = pltpu.roll(v, n - 1, axis)
    idx = lax.broadcasted_iota(jnp.int32, v.shape, axis)
    return jnp.where(idx == n - 1, 0.0, r)


def shift_bwd(v, axis):
    r = pltpu.roll(v, 1, axis)
    idx = lax.broadcasted_iota(jnp.int32, v.shape, axis)
    return jnp.where(idx == 0, 0.0, r)


def stencil_kernel(count_ref, now_hbm, prev_hbm, adj_lo, adj_hi, mat_hbm, mat_lo, mat_hi, snap_hbm,
                   src_hbm, now_ref, prev_ref, img_ref, curb, oldb, matb, snapb, srcb, pbuf, qbuf,
                   wc, wzf, wzb, wxf, wxb, wyf, wyb, sems):
    ext = curb.shape[0]
    nx, ny = curb.shape[1], curb.shape[2]
    planes = ext - 2 * HALO
    steps = snapb.shape[0]
    count = count_ref[0]
    copies = []

    def fetch(src, dst):
        c = pltpu.make_async_copy(src, dst, sems.at[len(copies)])
        c.start()
        copies.append(c)
        return c

    inner_at, lo_at, hi_at = pl.ds(HALO, planes), pl.ds(0, HALO), pl.ds(HALO + planes, HALO)
    need_mat = [fetch(mat_hbm, matb.at[:, inner_at]), fetch(mat_lo, matb.at[:, lo_at]),
                fetch(mat_hi, matb.at[:, hi_at])]
    need_adj = [fetch(now_hbm, curb.at[inner_at]), fetch(adj_lo.at[0], curb.at[lo_at]),
                fetch(adj_hi.at[0], curb.at[hi_at]), fetch(prev_hbm, oldb.at[inner_at]),
                fetch(adj_lo.at[1], oldb.at[lo_at]), fetch(adj_hi.at[1], oldb.at[hi_at]),
                fetch(src_hbm, srcb)]
    need_snap = [fetch(snap_hbm.at[steps - 1 - step], snapb.at[steps - 1 - step])
                 for step in range(steps)]
    for c in need_mat:
        c.wait()

    def weights(e, carry):
        bc = matb[1, e]
        kap = 0.08 * matb[0, e]
        zf = 0.5 * (bc + matb[1, e + 1])
        zb = 0.5 * (matb[1, jnp.maximum(e - 1, 0)] + bc)
        xf = 0.5 * (bc + shift_fwd(bc, 0, nx))
        xb = 0.5 * (shift_bwd(bc, 0) + bc)
        yf = 0.5 * (bc + shift_fwd(bc, 1, ny))
        yb = 0.5 * (shift_bwd(bc, 1) + bc)
        xi = lax.broadcasted_iota(jnp.int32, bc.shape, 0)
        yi = lax.broadcasted_iota(jnp.int32, bc.shape, 1)
        wc[e] = 2.0 - kap * (((zf + zb) + (xf + xb)) + (yf + yb))
        wzf[e] = kap * zf
        wzb[e] = kap * zb
        wxf[e] = jnp.where(xi == nx - 1, 0.0, kap * xf)
        wxb[e] = jnp.where(xi == 0, 0.0, kap * xb)
        wyf[e] = jnp.where(yi == ny - 1, 0.0, kap * yf)
        wyb[e] = jnp.where(yi == 0, 0.0, kap * yb)
        return carry

    lax.fori_loop(0, ext - 1, weights, 0)
    for c in need_adj:
        c.wait()

    def one_step(step, cur, old, dst, lo, hi):
        moment = steps - 1 - step
        need_snap[step].wait()

        def plane(e, with_source):
            pc = cur(e)
            new = wc[e] * pc + wzf[e] * cur(e + 1)
            new = new + wzb[e] * cur(e - 1)
            new = new + wxf[e] * pltpu.roll(pc, nx - 1, 0)
            new = new + wxb[e] * pltpu.roll(pc, 1, 0)
            new = new + wyf[e] * pltpu.roll(pc, ny - 1, 1)
            new = new + wyb[e] * pltpu.roll(pc, 1, 1)
            new = new - old(e)
            if with_source:
                new = new + 0.08 * srcb[moment]
            dst(e, new)
            inner = jnp.logical_and(e >= HALO, e < ext - HALO)

            @pl.when(inner)
            def _():
                z = e - HALO
                gained = snapb[moment, z].astype(jnp.float32) * new
                if step == 0:
                    img_ref[z] = gained
                elif step == steps - 1:
                    img_ref[z] = count * (img_ref[z] + gained)
                else:
                    img_ref[z] = img_ref[z] + gained

        def plain(e, carry):
            plane(e, False)
            return carry

        at_source = HALO + 2
        lax.fori_loop(lo, at_source, plain, 0)
        plane(at_source, True)
        lax.fori_loop(at_source + 1, hi, plain, 0)

    def rd(ref):
        return lambda e: ref[e]

    def wr(ref):
        def f(e, v):
            ref[e] = v

        return f

    def wr_inner(ref, out):
        def f(e, v):
            ref[e] = v

            @pl.when(jnp.logical_and(e >= HALO, e < ext - HALO))
            def _():
                out[e - HALO] = v

        return f

    def wr_out(out):
        def f(e, v):
            out[e - HALO] = v

        return f

    one_step(0, rd(curb), rd(oldb), wr(pbuf), 1, ext - 1)
    one_step(1, rd(pbuf), rd(curb), wr(qbuf), 2, ext - 2)
    one_step(2, rd(qbuf), rd(pbuf), wr_inner(pbuf, prev_ref), 3, ext - 3)
    one_step(3, rd(pbuf), rd(qbuf), wr_out(now_ref), HALO, ext - HALO)


def run_steps(count, adj_now, adj_prev, adj_lo, adj_hi, mat, mat_lo, mat_hi, snaps, src):
    planes, nx, ny = adj_now.shape
    ext = planes + 2 * HALO
    steps = snaps.shape[0]
    vmem = pltpu.VMEM
    out_shape = [jax.ShapeDtypeStruct((planes, nx, ny), jnp.float32)] * 3
    field = pltpu.VMEM((ext, nx, ny), jnp.float32)
    return pl.pallas_call(
        stencil_kernel,
        out_shape=out_shape,
        in_specs=[pl.BlockSpec(memory_space=pltpu.SMEM)] + [pl.BlockSpec(memory_space=pl.ANY)] * 9,
        out_specs=[pl.BlockSpec(memory_space=vmem)] * 3,
        scratch_shapes=[field, field, pltpu.VMEM((2, ext, nx, ny), jnp.float32),
                        pltpu.VMEM(snaps.shape, snaps.dtype), pltpu.VMEM(src.shape, jnp.float32)]
        + [field] * 9 + [pltpu.SemaphoreType.DMA((10 + steps,))],
        compiler_params=pltpu.CompilerParams(vmem_limit_bytes=56 * 1024 * 1024),
        interpret=INTERPRET,
    )(count, adj_now, adj_prev, adj_lo, adj_hi, mat, mat_lo, mat_hi, snaps, src)


def halo_of(shard, axis, dim, width):
    peers, length = (lax.axis_size(axis), shard.shape[dim])
    up = [(i, (i + 1) % peers) for i in range(peers - 1)]
    down = [(j, i) for i, j in up]
    last = lax.slice_in_dim(shard, length - width, length, axis=dim)
    first = lax.slice_in_dim(shard, 0, width, axis=dim)
    return lax.ppermute(last, axis, up), lax.ppermute(first, axis, down)


def bit_order(peers):
    return list(range(peers.bit_length() - 1))


def gather_rows(shard, axis, dim):
    peers = lax.axis_size(axis)
    me = lax.axis_index(axis)
    pieces = jnp.expand_dims(shard, dim)
    for b in reversed(bit_order(peers)):
        pairs = [(i, i ^ (1 << b)) for i in range(peers)]
        got = lax.ppermute(pieces, axis, pairs)
        mine = (me >> b) & 1
        lo = jnp.where(mine == 0, pieces, got)
        hi = jnp.where(mine == 0, got, pieces)
        both = jnp.stack([lo, hi], axis=dim + 1)
        shape = list(pieces.shape)
        shape[dim] = shape[dim] * 2
        pieces = both.reshape(shape)
    shape = list(shard.shape)
    shape[dim] = shape[dim] * peers
    return pieces.reshape(shape)


def scatter_rows(full, axis, dim):
    peers = lax.axis_size(axis)
    me = lax.axis_index(axis)
    nbits = peers.bit_length() - 1
    rows = full.shape[dim] // peers
    shape = list(full.shape)
    blocks = full.reshape(shape[:dim] + [2] * nbits + [rows] + shape[dim + 1:])
    for b in bit_order(peers):
        where = dim + (nbits - 1 - b)
        mine = (me >> b) & 1
        keep = lax.dynamic_index_in_dim(blocks, mine, axis=where, keepdims=False)
        send = lax.dynamic_index_in_dim(blocks, 1 - mine, axis=where, keepdims=False)
        pairs = [(i, i ^ (1 << b)) for i in range(peers)]
        got = lax.ppermute(send, axis, pairs)
        blocks = keep + got
    return blocks


def source_plane(rows_x, rows_y, amounts, width_x, width_y):
    onehot_x = (rows_x[:, None] == jnp.arange(width_x, dtype=jnp.int32)[None, :]).astype(
        jnp.float32
    )
    onehot_y = (rows_y[:, None] == jnp.arange(width_y, dtype=jnp.int32)[None, :]).astype(
        jnp.float32
    )
    return jnp.dot((onehot_x * amounts[:, None]).T, onehot_y, precision=lax.Precision.HIGHEST)


def body(adj_now, adj_prev, fwd_snap, velocity, density, shot_count, rec_x, rec_y, residual):
    width_x = adj_now.shape[2]
    width_y = adj_now.shape[3]
    steps = fwd_snap.shape[1]
    groups = lax.axis_size("shots")
    adj_lo, adj_hi = halo_of(jnp.stack([adj_now[0], adj_prev[0]]), "depth", 1, HALO)
    local = jnp.stack([density * velocity * velocity, 1.0 / density])
    packed = gather_rows(local, "shots", 2)
    mat_lo, mat_hi = halo_of(packed, "depth", 1, HALO)
    holds_source = (lax.axis_index("depth") == 0).astype(jnp.float32)
    src = jnp.stack(
        [source_plane(rec_x[0], rec_y[0], residual[0, t], width_x, width_y) for t in range(steps)]
    ) * holds_source
    count = shot_count.astype(jnp.float32)
    current, older, weighted = run_steps(
        count, adj_now[0], adj_prev[0], adj_lo, adj_hi, packed, mat_lo, mat_hi, fwd_snap[0], src
    )
    summed = scatter_rows(weighted, "shots", 1)
    grad_vel = 2.0 * density * velocity * summed / (4.0 * groups)
    return (current[None], older[None], grad_vel)


def solution(mesh):
    in_specs = (
        P("shots", "depth", None, None),
        P("shots", "depth", None, None),
        P("shots", None, "depth", None, None),
        P("depth", "shots", None),
        P("depth", "shots", None),
        P("shots"),
        P("shots", None),
        P("shots", None),
        P("shots", None, None),
    )
    out_specs = (
        P("shots", "depth", None, None),
        P("shots", "depth", None, None),
        P("depth", "shots", None),
    )
    return jax.shard_map(body, mesh=mesh, in_specs=in_specs, out_specs=out_specs, check_vma=False)
```

```python
import jax
import jax.numpy as jnp
from jax import lax
from jax.sharding import PartitionSpec as P
from jax.experimental import pallas as pl
from jax.experimental.pallas import tpu as pltpu

INTERPRET = False

HALO = 4


def stencil_kernel(count_ref, now_hbm, prev_hbm, adj_lo, adj_hi, mat_hbm, mat_lo, mat_hi, snap_hbm,
                   src_hbm, now_ref, prev_ref, img_ref, curb, oldb, matb, snapb, srcb, pbuf, qbuf,
                   wc, wzf, wzb, wxf, wxb, wyf, wyb, sems):
    ext = curb.shape[0]
    nx, ny = curb.shape[1], curb.shape[2]
    planes = ext - 2 * HALO
    steps = snapb.shape[0]
    count = count_ref[0]
    copies = []

    def fetch(src, dst):
        c = pltpu.make_async_copy(src, dst, sems.at[len(copies)])
        c.start()
        copies.append(c)
        return c

    inner_at, lo_at, hi_at = pl.ds(HALO, planes), pl.ds(0, HALO), pl.ds(HALO + planes, HALO)
    need_mat = [fetch(mat_hbm, matb.at[:, inner_at]), fetch(mat_lo, matb.at[:, lo_at]),
                fetch(mat_hi, matb.at[:, hi_at])]
    need_adj = [fetch(now_hbm, curb.at[inner_at]), fetch(adj_lo.at[0], curb.at[lo_at]),
                fetch(adj_hi.at[0], curb.at[hi_at]), fetch(prev_hbm, oldb.at[inner_at]),
                fetch(adj_lo.at[1], oldb.at[lo_at]), fetch(adj_hi.at[1], oldb.at[hi_at]),
                fetch(src_hbm, srcb)]
    need_snap = [fetch(snap_hbm.at[steps - 1 - step], snapb.at[steps - 1 - step])
                 for step in range(steps)]
    for c in need_mat:
        c.wait()

    rows = 8
    chunks = nx // rows
    sub = lax.broadcasted_iota(jnp.int32, (rows, ny), 0)
    lane = lax.broadcasted_iota(jnp.int32, (rows, ny), 1)

    def around(get, c):
        mid = get(pl.ds(c * rows, rows))
        up = get(pl.ds(max(c - 1, 0) * rows, rows))
        down = get(pl.ds(min(c + 1, chunks - 1) * rows, rows))
        ahead = jnp.where(sub == rows - 1, pltpu.roll(down, rows - 1, 0), pltpu.roll(mid, rows - 1, 0))
        behind = jnp.where(sub == 0, pltpu.roll(up, 1, 0), pltpu.roll(mid, 1, 0))
        return mid, ahead, behind

    def weights(e, carry):
        for c in range(chunks):
            r = pl.ds(c * rows, rows)
            bc, bxa, bxb = around(lambda q: matb[1, e, q], c)
            xi = sub + c * rows
            kap = 0.08 * matb[0, e, r]
            zf = 0.5 * (bc + matb[1, e + 1, r])
            zb = 0.5 * (matb[1, jnp.maximum(e - 1, 0), r] + bc)
            xf = 0.5 * (bc + jnp.where(xi == nx - 1, 0.0, bxa))
            xb = 0.5 * (jnp.where(xi == 0, 0.0, bxb) + bc)
            yf = 0.5 * (bc + jnp.where(lane == ny - 1, 0.0, pltpu.roll(bc, ny - 1, 1)))
            yb = 0.5 * (jnp.where(lane == 0, 0.0, pltpu.roll(bc, 1, 1)) + bc)
            wc[e, r] = 2.0 - kap * (((zf + zb) + (xf + xb)) + (yf + yb))
            wzf[e, r] = kap * zf
            wzb[e, r] = kap * zb
            wxf[e, r] = jnp.where(xi == nx - 1, 0.0, kap * xf)
            wxb[e, r] = jnp.where(xi == 0, 0.0, kap * xb)
            wyf[e, r] = jnp.where(lane == ny - 1, 0.0, kap * yf)
            wyb[e, r] = jnp.where(lane == 0, 0.0, kap * yb)
        return carry

    lax.fori_loop(0, ext - 1, weights, 0)
    for c in need_adj:
        c.wait()

    def one_step(step, cur, old, dst, lo, hi):
        moment = steps - 1 - step
        need_snap[step].wait()

        def plane(e, with_source):
            inner = jnp.logical_and(e >= HALO, e < ext - HALO)
            for c in range(chunks):
                r = pl.ds(c * rows, rows)
                pc, pxa, pxb = around(lambda q: cur(e, q), c)
                new = wc[e, r] * pc + wzf[e, r] * cur(e + 1, r)
                new = new + wzb[e, r] * cur(e - 1, r)
                new = new + wxf[e, r] * pxa
                new = new + wxb[e, r] * pxb
                new = new + wyf[e, r] * pltpu.roll(pc, ny - 1, 1)
                new = new + wyb[e, r] * pltpu.roll(pc, 1, 1)
                new = new - old(e, r)
                if with_source:
                    new = new + 0.08 * srcb[moment, r]
                dst(e, r, new)

                @pl.when(inner)
                def _():
                    z = e - HALO
                    gained = snapb[moment, z, r].astype(jnp.float32) * new
                    if step == 0:
                        img_ref[z, r] = gained
                    elif step == steps - 1:
                        img_ref[z, r] = count * (img_ref[z, r] + gained)
                    else:
                        img_ref[z, r] = img_ref[z, r] + gained

        def plain(e, carry):
            plane(e, False)
            return carry

        at_source = HALO + 2
        lax.fori_loop(lo, at_source, plain, 0)
        plane(at_source, True)
        lax.fori_loop(at_source + 1, hi, plain, 0)

    def rd(ref):
        return lambda e, r: ref[e, r]

    def wr(ref):
        def f(e, r, v):
            ref[e, r] = v

        return f

    def wr_inner(ref, out):
        def f(e, r, v):
            ref[e, r] = v

            @pl.when(jnp.logical_and(e >= HALO, e < ext - HALO))
            def _():
                out[e - HALO, r] = v

        return f

    def wr_out(out):
        def f(e, r, v):
            out[e - HALO, r] = v

        return f

    one_step(0, rd(curb), rd(oldb), wr(pbuf), 1, ext - 1)
    one_step(1, rd(pbuf), rd(curb), wr(qbuf), 2, ext - 2)
    one_step(2, rd(qbuf), rd(pbuf), wr_inner(pbuf, prev_ref), 3, ext - 3)
    one_step(3, rd(pbuf), rd(qbuf), wr_out(now_ref), HALO, ext - HALO)


def run_steps(count, adj_now, adj_prev, adj_lo, adj_hi, mat, mat_lo, mat_hi, snaps, src):
    planes, nx, ny = adj_now.shape
    ext = planes + 2 * HALO
    steps = snaps.shape[0]
    vmem = pltpu.VMEM
    out_shape = [jax.ShapeDtypeStruct((planes, nx, ny), jnp.float32)] * 3
    field = pltpu.VMEM((ext, nx, ny), jnp.float32)
    return pl.pallas_call(
        stencil_kernel,
        out_shape=out_shape,
        in_specs=[pl.BlockSpec(memory_space=pltpu.SMEM)] + [pl.BlockSpec(memory_space=pl.ANY)] * 9,
        out_specs=[pl.BlockSpec(memory_space=vmem)] * 3,
        scratch_shapes=[field, field, pltpu.VMEM((2, ext, nx, ny), jnp.float32),
                        pltpu.VMEM(snaps.shape, snaps.dtype), pltpu.VMEM(src.shape, jnp.float32)]
        + [field] * 9 + [pltpu.SemaphoreType.DMA((10 + steps,))],
        compiler_params=pltpu.CompilerParams(vmem_limit_bytes=56 * 1024 * 1024),
        interpret=INTERPRET,
    )(count, adj_now, adj_prev, adj_lo, adj_hi, mat, mat_lo, mat_hi, snaps, src)


def halo_of(shard, axis, dim, width):
    peers, length = (lax.axis_size(axis), shard.shape[dim])
    up = [(i, (i + 1) % peers) for i in range(peers - 1)]
    down = [(j, i) for i, j in up]
    last = lax.slice_in_dim(shard, length - width, length, axis=dim)
    first = lax.slice_in_dim(shard, 0, width, axis=dim)
    return lax.ppermute(last, axis, up), lax.ppermute(first, axis, down)


def bit_order(peers):
    return list(range(peers.bit_length() - 1))


def gather_rows(shard, axis, dim):
    peers = lax.axis_size(axis)
    me = lax.axis_index(axis)
    pieces = jnp.expand_dims(shard, dim)
    for b in reversed(bit_order(peers)):
        pairs = [(i, i ^ (1 << b)) for i in range(peers)]
        got = lax.ppermute(pieces, axis, pairs)
        mine = (me >> b) & 1
        lo = jnp.where(mine == 0, pieces, got)
        hi = jnp.where(mine == 0, got, pieces)
        both = jnp.stack([lo, hi], axis=dim + 1)
        shape = list(pieces.shape)
        shape[dim] = shape[dim] * 2
        pieces = both.reshape(shape)
    shape = list(shard.shape)
    shape[dim] = shape[dim] * peers
    return pieces.reshape(shape)


def scatter_rows(full, axis, dim):
    peers = lax.axis_size(axis)
    me = lax.axis_index(axis)
    nbits = peers.bit_length() - 1
    rows = full.shape[dim] // peers
    shape = list(full.shape)
    blocks = full.reshape(shape[:dim] + [2] * nbits + [rows] + shape[dim + 1:])
    for b in bit_order(peers):
        where = dim + (nbits - 1 - b)
        mine = (me >> b) & 1
        keep = lax.dynamic_index_in_dim(blocks, mine, axis=where, keepdims=False)
        send = lax.dynamic_index_in_dim(blocks, 1 - mine, axis=where, keepdims=False)
        pairs = [(i, i ^ (1 << b)) for i in range(peers)]
        got = lax.ppermute(send, axis, pairs)
        blocks = keep + got
    return blocks


def source_plane(rows_x, rows_y, amounts, width_x, width_y):
    onehot_x = (rows_x[:, None] == jnp.arange(width_x, dtype=jnp.int32)[None, :]).astype(
        jnp.float32
    )
    onehot_y = (rows_y[:, None] == jnp.arange(width_y, dtype=jnp.int32)[None, :]).astype(
        jnp.float32
    )
    return jnp.dot((onehot_x * amounts[:, None]).T, onehot_y, precision=lax.Precision.HIGHEST)


def body(adj_now, adj_prev, fwd_snap, velocity, density, shot_count, rec_x, rec_y, residual):
    width_x = adj_now.shape[2]
    width_y = adj_now.shape[3]
    steps = fwd_snap.shape[1]
    groups = lax.axis_size("shots")
    adj_lo, adj_hi = halo_of(jnp.stack([adj_now[0], adj_prev[0]]), "depth", 1, HALO)
    local = jnp.stack([density * velocity * velocity, 1.0 / density])
    packed = gather_rows(local, "shots", 2)
    mat_lo, mat_hi = halo_of(packed, "depth", 1, HALO)
    holds_source = (lax.axis_index("depth") == 0).astype(jnp.float32)
    src = jnp.stack(
        [source_plane(rec_x[0], rec_y[0], residual[0, t], width_x, width_y) for t in range(steps)]
    ) * holds_source
    count = shot_count.astype(jnp.float32)
    current, older, weighted = run_steps(
        count, adj_now[0], adj_prev[0], adj_lo, adj_hi, packed, mat_lo, mat_hi, fwd_snap[0], src
    )
    summed = scatter_rows(weighted, "shots", 1)
    grad_vel = 2.0 * density * velocity * summed / (4.0 * groups)
    return (current[None], older[None], grad_vel)


def solution(mesh):
    in_specs = (
        P("shots", "depth", None, None),
        P("shots", "depth", None, None),
        P("shots", None, "depth", None, None),
        P("depth", "shots", None),
        P("depth", "shots", None),
        P("shots"),
        P("shots", None),
        P("shots", None),
        P("shots", None, None),
    )
    out_specs = (
        P("shots", "depth", None, None),
        P("shots", "depth", None, None),
        P("depth", "shots", None),
    )
    return jax.shard_map(body, mesh=mesh, in_specs=in_specs, out_specs=out_specs, check_vma=False)
```

```python
import jax
import jax.numpy as jnp
from jax import lax
from jax.sharding import PartitionSpec as P
from jax.experimental import pallas as pl
from jax.experimental.pallas import tpu as pltpu

INTERPRET = False

HALO = 4


def shift_fwd(v, axis, n):
    r = pltpu.roll(v, n - 1, axis)
    idx = lax.broadcasted_iota(jnp.int32, v.shape, axis)
    return jnp.where(idx == n - 1, 0.0, r)


def shift_bwd(v, axis):
    r = pltpu.roll(v, 1, axis)
    idx = lax.broadcasted_iota(jnp.int32, v.shape, axis)
    return jnp.where(idx == 0, 0.0, r)


def stencil_kernel(count_ref, now_hbm, prev_hbm, adj_lo, adj_hi, mat_hbm, mat_lo, mat_hi, snap_hbm,
                   src_hbm, now_ref, prev_ref, img_ref, curb, oldb, matb, snapb, srcb, pbuf, qbuf,
                   kz, kxf, kxb, kyf, kyb, kk, sems):
    ext = curb.shape[0]
    nx, ny = curb.shape[1], curb.shape[2]
    planes = ext - 2 * HALO
    steps = snapb.shape[0]
    count = count_ref[0]
    copies = []

    def fetch(src, dst):
        c = pltpu.make_async_copy(src, dst, sems.at[len(copies)])
        c.start()
        copies.append(c)
        return c

    inner_at, lo_at, hi_at = pl.ds(HALO, planes), pl.ds(0, HALO), pl.ds(HALO + planes, HALO)
    need_mat = [fetch(mat_hbm, matb.at[:, inner_at]), fetch(mat_lo, matb.at[:, lo_at]),
                fetch(mat_hi, matb.at[:, hi_at])]
    need_adj = [fetch(now_hbm, curb.at[inner_at]), fetch(adj_lo.at[0], curb.at[lo_at]),
                fetch(adj_hi.at[0], curb.at[hi_at]), fetch(prev_hbm, oldb.at[inner_at]),
                fetch(adj_lo.at[1], oldb.at[lo_at]), fetch(adj_hi.at[1], oldb.at[hi_at]),
                fetch(src_hbm, srcb)]
    need_snap = [fetch(snap_hbm.at[steps - 1 - step], snapb.at[steps - 1 - step])
                 for step in range(steps)]
    for c in need_mat:
        c.wait()

    def weights(e, carry):
        bc = matb[1, e]
        kz[e] = 0.5 * (bc + matb[1, e + 1])
        kxf[e] = 0.5 * (bc + shift_fwd(bc, 0, nx))
        kxb[e] = 0.5 * (shift_bwd(bc, 0) + bc)
        kyf[e] = 0.5 * (bc + shift_fwd(bc, 1, ny))
        kyb[e] = 0.5 * (shift_bwd(bc, 1) + bc)
        kk[e] = 0.08 * matb[0, e]
        return carry

    lax.fori_loop(0, ext - 1, weights, 0)
    for c in need_adj:
        c.wait()

    def one_step(step, cur, old, dst, lo, hi):
        moment = steps - 1 - step
        need_snap[step].wait()

        def plane(e, carry):
            pc = cur(e)
            total = kz[e] * (cur(e + 1) - pc) - kz[e - 1] * (pc - cur(e - 1))
            total = total + (kxf[e] * (shift_fwd(pc, 0, nx) - pc) - kxb[e] * (pc - shift_bwd(pc, 0)))
            total = total + (kyf[e] * (shift_fwd(pc, 1, ny) - pc) - kyb[e] * (pc - shift_bwd(pc, 1)))
            weight = jnp.where(e == HALO + 2, 1.0, 0.0)
            new = 2.0 * pc - old(e) + kk[e] * total + 0.08 * srcb[moment] * weight
            dst(e, new)
            inner = jnp.logical_and(e >= HALO, e < ext - HALO)

            @pl.when(inner)
            def _():
                z = e - HALO
                gained = snapb[moment, z].astype(jnp.float32) * new
                if step == 0:
                    img_ref[z] = gained
                elif step == steps - 1:
                    img_ref[z] = count * (img_ref[z] + gained)
                else:
                    img_ref[z] = img_ref[z] + gained

            return carry

        lax.fori_loop(lo, hi, plane, 0)

    def rd(ref):
        return lambda e: ref[e]

    def wr(ref):
        def f(e, v):
            ref[e] = v

        return f

    def wr_inner(ref, out):
        def f(e, v):
            ref[e] = v

            @pl.when(jnp.logical_and(e >= HALO, e < ext - HALO))
            def _():
                out[e - HALO] = v

        return f

    def wr_out(out):
        def f(e, v):
            out[e - HALO] = v

        return f

    one_step(0, rd(curb), rd(oldb), wr(pbuf), 1, ext - 1)
    one_step(1, rd(pbuf), rd(curb), wr(qbuf), 2, ext - 2)
    one_step(2, rd(qbuf), rd(pbuf), wr_inner(pbuf, prev_ref), 3, ext - 3)
    one_step(3, rd(pbuf), rd(qbuf), wr_out(now_ref), HALO, ext - HALO)


def run_steps(count, adj_now, adj_prev, adj_lo, adj_hi, mat, mat_lo, mat_hi, snaps, src):
    planes, nx, ny = adj_now.shape
    ext = planes + 2 * HALO
    steps = snaps.shape[0]
    vmem = pltpu.VMEM
    out_shape = [jax.ShapeDtypeStruct((planes, nx, ny), jnp.float32)] * 3
    field = pltpu.VMEM((ext, nx, ny), jnp.float32)
    return pl.pallas_call(
        stencil_kernel,
        out_shape=out_shape,
        in_specs=[pl.BlockSpec(memory_space=pltpu.SMEM)] + [pl.BlockSpec(memory_space=pl.ANY)] * 9,
        out_specs=[pl.BlockSpec(memory_space=vmem)] * 3,
        scratch_shapes=[field, field, pltpu.VMEM((2, ext, nx, ny), jnp.float32),
                        pltpu.VMEM(snaps.shape, snaps.dtype), pltpu.VMEM(src.shape, jnp.float32)]
        + [field] * 8 + [pltpu.SemaphoreType.DMA((10 + steps,))],
        compiler_params=pltpu.CompilerParams(vmem_limit_bytes=56 * 1024 * 1024),
        interpret=INTERPRET,
    )(count, adj_now, adj_prev, adj_lo, adj_hi, mat, mat_lo, mat_hi, snaps, src)


def halo_of(shard, axis, dim, width):
    peers, length = (lax.axis_size(axis), shard.shape[dim])
    up = [(i, (i + 1) % peers) for i in range(peers - 1)]
    down = [(j, i) for i, j in up]
    last = lax.slice_in_dim(shard, length - width, length, axis=dim)
    first = lax.slice_in_dim(shard, 0, width, axis=dim)
    return lax.ppermute(last, axis, up), lax.ppermute(first, axis, down)


def bit_order(peers):
    return list(range(peers.bit_length() - 1))


def gather_rows(shard, axis, dim):
    peers = lax.axis_size(axis)
    me = lax.axis_index(axis)
    pieces = jnp.expand_dims(shard, dim)
    for b in reversed(bit_order(peers)):
        pairs = [(i, i ^ (1 << b)) for i in range(peers)]
        got = lax.ppermute(pieces, axis, pairs)
        mine = (me >> b) & 1
        lo = jnp.where(mine == 0, pieces, got)
        hi = jnp.where(mine == 0, got, pieces)
        both = jnp.stack([lo, hi], axis=dim + 1)
        shape = list(pieces.shape)
        shape[dim] = shape[dim] * 2
        pieces = both.reshape(shape)
    shape = list(shard.shape)
    shape[dim] = shape[dim] * peers
    return pieces.reshape(shape)


def scatter_rows(full, axis, dim):
    peers = lax.axis_size(axis)
    me = lax.axis_index(axis)
    nbits = peers.bit_length() - 1
    rows = full.shape[dim] // peers
    shape = list(full.shape)
    blocks = full.reshape(shape[:dim] + [2] * nbits + [rows] + shape[dim + 1:])
    for b in bit_order(peers):
        where = dim + (nbits - 1 - b)
        mine = (me >> b) & 1
        keep = lax.dynamic_index_in_dim(blocks, mine, axis=where, keepdims=False)
        send = lax.dynamic_index_in_dim(blocks, 1 - mine, axis=where, keepdims=False)
        pairs = [(i, i ^ (1 << b)) for i in range(peers)]
        got = lax.ppermute(send, axis, pairs)
        blocks = keep + got
    return blocks


def source_plane(rows_x, rows_y, amounts, width_x, width_y):
    onehot_x = (rows_x[:, None] == jnp.arange(width_x, dtype=jnp.int32)[None, :]).astype(
        jnp.float32
    )
    onehot_y = (rows_y[:, None] == jnp.arange(width_y, dtype=jnp.int32)[None, :]).astype(
        jnp.float32
    )
    return jnp.dot((onehot_x * amounts[:, None]).T, onehot_y, precision=lax.Precision.HIGHEST)


def split_halo(shard, width):
    depth, shots = lax.axis_size("depth"), lax.axis_size("shots")
    core = lax.axis_index("shots") % 2
    length = shard.shape[1]
    start = jnp.where(core == 0, length - width, 0)
    sent = lax.dynamic_slice_in_dim(shard, start, width, axis=1)
    pairs = []
    for d in range(depth):
        for s in range(shots):
            to = d + 1 if s % 2 == 0 else d - 1
            if 0 <= to < depth:
                pairs.append((d * shots + s, to * shots + s))
    got = lax.ppermute(sent, ("depth", "shots"), pairs)
    other = lax.ppermute(got, "shots", [(s, s ^ 1) for s in range(shots)])
    lo = jnp.where(core == 0, got, other)
    hi = jnp.where(core == 0, other, got)
    return lo, hi


def body(adj_now, adj_prev, fwd_snap, velocity, density, shot_count, rec_x, rec_y, residual):
    width_x = adj_now.shape[2]
    width_y = adj_now.shape[3]
    steps = fwd_snap.shape[1]
    groups = lax.axis_size("shots")
    adj_lo, adj_hi = halo_of(jnp.stack([adj_now[0], adj_prev[0]]), "depth", 1, HALO)
    local = jnp.stack([density * velocity * velocity, 1.0 / density])
    packed = gather_rows(local, "shots", 2)
    mat_lo, mat_hi = split_halo(packed, HALO)
    holds_source = (lax.axis_index("depth") == 0).astype(jnp.float32)
    src = jnp.stack(
        [source_plane(rec_x[0], rec_y[0], residual[0, t], width_x, width_y) for t in range(steps)]
    ) * holds_source
    count = shot_count.astype(jnp.float32)
    current, older, weighted = run_steps(
        count, adj_now[0], adj_prev[0], adj_lo, adj_hi, packed, mat_lo, mat_hi, fwd_snap[0], src
    )
    summed = scatter_rows(weighted, "shots", 1)
    grad_vel = 2.0 * density * velocity * summed / (4.0 * groups)
    return (current[None], older[None], grad_vel)


def solution(mesh):
    in_specs = (
        P("shots", "depth", None, None),
        P("shots", "depth", None, None),
        P("shots", None, "depth", None, None),
        P("depth", "shots", None),
        P("depth", "shots", None),
        P("shots"),
        P("shots", None),
        P("shots", None),
        P("shots", None, None),
    )
    out_specs = (
        P("shots", "depth", None, None),
        P("shots", "depth", None, None),
        P("depth", "shots", None),
    )
    return jax.shard_map(body, mesh=mesh, in_specs=in_specs, out_specs=out_specs, check_vma=False)
```

```python
import jax
import jax.numpy as jnp
from jax import lax
from jax.sharding import PartitionSpec as P
from jax.experimental import pallas as pl
from jax.experimental.pallas import tpu as pltpu

INTERPRET = False

HALO = 4


def shift_fwd(v, axis, n):
    r = pltpu.roll(v, n - 1, axis)
    idx = lax.broadcasted_iota(jnp.int32, v.shape, axis)
    return jnp.where(idx == n - 1, 0.0, r)


def shift_bwd(v, axis):
    r = pltpu.roll(v, 1, axis)
    idx = lax.broadcasted_iota(jnp.int32, v.shape, axis)
    return jnp.where(idx == 0, 0.0, r)


def stencil_kernel(count_ref, now_hbm, prev_hbm, adj_lo, adj_hi, mat_hbm, mat_lo, mat_hi, snap_hbm,
                   src_hbm, now_ref, prev_ref, img_ref, curb, oldb, matb, snapb, srcb, pbuf, qbuf,
                   kz, kxf, kxb, kyf, kyb, kk, sems):
    ext = curb.shape[0]
    nx, ny = curb.shape[1], curb.shape[2]
    planes = ext - 2 * HALO
    steps = snapb.shape[0]
    count = count_ref[0]
    copies = []

    def fetch(src, dst):
        c = pltpu.make_async_copy(src, dst, sems.at[len(copies)])
        c.start()
        copies.append(c)
        return c

    inner_at, lo_at, hi_at = pl.ds(HALO, planes), pl.ds(0, HALO), pl.ds(HALO + planes, HALO)
    need_mat = [fetch(mat_hbm, matb.at[:, inner_at])]
    own = pltpu.make_async_copy(mat_lo, matb.at[:, lo_at], sems.at[10 + steps])
    swapped = pltpu.make_async_copy(mat_hi, matb.at[:, hi_at], sems.at[11 + steps])

    @pl.when(count_ref[1] == 0.0)
    def _():
        own.start()
        swapped.start()

    @pl.when(count_ref[1] != 0.0)
    def _():
        pltpu.make_async_copy(mat_lo, matb.at[:, hi_at], sems.at[11 + steps]).start()
        pltpu.make_async_copy(mat_hi, matb.at[:, lo_at], sems.at[10 + steps]).start()

    need_mat += [own, swapped]
    need_adj = [fetch(now_hbm, curb.at[inner_at]), fetch(adj_lo.at[0], curb.at[lo_at]),
                fetch(adj_hi.at[0], curb.at[hi_at]), fetch(prev_hbm, oldb.at[inner_at]),
                fetch(adj_lo.at[1], oldb.at[lo_at]), fetch(adj_hi.at[1], oldb.at[hi_at]),
                fetch(src_hbm, srcb)]
    need_snap = [fetch(snap_hbm.at[steps - 1 - step], snapb.at[steps - 1 - step])
                 for step in range(steps)]
    for c in need_mat:
        c.wait()

    def weights(e, carry):
        bc = matb[1, e]
        kz[e] = 0.5 * (bc + matb[1, e + 1])
        kxf[e] = 0.5 * (bc + shift_fwd(bc, 0, nx))
        kxb[e] = 0.5 * (shift_bwd(bc, 0) + bc)
        kyf[e] = 0.5 * (bc + shift_fwd(bc, 1, ny))
        kyb[e] = 0.5 * (shift_bwd(bc, 1) + bc)
        kk[e] = 0.08 * matb[0, e]
        return carry

    lax.fori_loop(0, ext - 1, weights, 0)
    for c in need_adj:
        c.wait()

    def one_step(step, cur, old, dst, lo, hi):
        moment = steps - 1 - step
        need_snap[step].wait()

        def plane(e, carry):
            pc = cur(e)
            total = kz[e] * (cur(e + 1) - pc) - kz[e - 1] * (pc - cur(e - 1))
            total = total + (kxf[e] * (shift_fwd(pc, 0, nx) - pc) - kxb[e] * (pc - shift_bwd(pc, 0)))
            total = total + (kyf[e] * (shift_fwd(pc, 1, ny) - pc) - kyb[e] * (pc - shift_bwd(pc, 1)))
            weight = jnp.where(e == HALO + 2, 1.0, 0.0)
            new = 2.0 * pc - old(e) + kk[e] * total + 0.08 * srcb[moment] * weight
            dst(e, new)
            inner = jnp.logical_and(e >= HALO, e < ext - HALO)

            @pl.when(inner)
            def _():
                z = e - HALO
                gained = snapb[moment, z].astype(jnp.float32) * new
                if step == 0:
                    img_ref[z] = gained
                elif step == steps - 1:
                    img_ref[z] = count * (img_ref[z] + gained)
                else:
                    img_ref[z] = img_ref[z] + gained

            return carry

        lax.fori_loop(lo, hi, plane, 0, unroll=2)

    def rd(ref):
        return lambda e: ref[e]

    def wr(ref):
        def f(e, v):
            ref[e] = v

        return f

    def wr_inner(ref, out):
        def f(e, v):
            ref[e] = v

            @pl.when(jnp.logical_and(e >= HALO, e < ext - HALO))
            def _():
                out[e - HALO] = v

        return f

    def wr_out(out):
        def f(e, v):
            out[e - HALO] = v

        return f

    one_step(0, rd(curb), rd(oldb), wr(pbuf), 1, ext - 1)
    one_step(1, rd(pbuf), rd(curb), wr(qbuf), 2, ext - 2)
    one_step(2, rd(qbuf), rd(pbuf), wr_inner(pbuf, prev_ref), 3, ext - 3)
    one_step(3, rd(pbuf), rd(qbuf), wr_out(now_ref), HALO, ext - HALO)


def run_steps(count, adj_now, adj_prev, adj_lo, adj_hi, mat, mat_lo, mat_hi, snaps, src):
    planes, nx, ny = adj_now.shape
    ext = planes + 2 * HALO
    steps = snaps.shape[0]
    vmem = pltpu.VMEM
    out_shape = [jax.ShapeDtypeStruct((planes, nx, ny), jnp.float32)] * 3
    field = pltpu.VMEM((ext, nx, ny), jnp.float32)
    return pl.pallas_call(
        stencil_kernel,
        out_shape=out_shape,
        in_specs=[pl.BlockSpec(memory_space=pltpu.SMEM)] + [pl.BlockSpec(memory_space=pl.ANY)] * 9,
        out_specs=[pl.BlockSpec(memory_space=vmem)] * 3,
        scratch_shapes=[field, field, pltpu.VMEM((2, ext, nx, ny), jnp.float32),
                        pltpu.VMEM(snaps.shape, snaps.dtype), pltpu.VMEM(src.shape, jnp.float32)]
        + [field] * 8 + [pltpu.SemaphoreType.DMA((12 + steps,))],
        compiler_params=pltpu.CompilerParams(vmem_limit_bytes=56 * 1024 * 1024),
        interpret=INTERPRET,
    )(count, adj_now, adj_prev, adj_lo, adj_hi, mat, mat_lo, mat_hi, snaps, src)


def halo_of(shard, axis, dim, width):
    peers, length = (lax.axis_size(axis), shard.shape[dim])
    up = [(i, (i + 1) % peers) for i in range(peers - 1)]
    down = [(j, i) for i, j in up]
    last = lax.slice_in_dim(shard, length - width, length, axis=dim)
    first = lax.slice_in_dim(shard, 0, width, axis=dim)
    return lax.ppermute(last, axis, up), lax.ppermute(first, axis, down)


def bit_order(peers):
    return list(range(peers.bit_length() - 1))


def gather_rows(shard, axis, dim):
    peers = lax.axis_size(axis)
    me = lax.axis_index(axis)
    pieces = jnp.expand_dims(shard, dim)
    for b in reversed(bit_order(peers)):
        pairs = [(i, i ^ (1 << b)) for i in range(peers)]
        got = lax.ppermute(pieces, axis, pairs)
        mine = (me >> b) & 1
        lo = jnp.where(mine == 0, pieces, got)
        hi = jnp.where(mine == 0, got, pieces)
        both = jnp.stack([lo, hi], axis=dim + 1)
        shape = list(pieces.shape)
        shape[dim] = shape[dim] * 2
        pieces = both.reshape(shape)
    shape = list(shard.shape)
    shape[dim] = shape[dim] * peers
    return pieces.reshape(shape)


def scatter_rows(full, axis, dim):
    peers = lax.axis_size(axis)
    me = lax.axis_index(axis)
    nbits = peers.bit_length() - 1
    rows = full.shape[dim] // peers
    shape = list(full.shape)
    blocks = full.reshape(shape[:dim] + [2] * nbits + [rows] + shape[dim + 1:])
    for b in bit_order(peers):
        where = dim + (nbits - 1 - b)
        mine = (me >> b) & 1
        keep = lax.dynamic_index_in_dim(blocks, mine, axis=where, keepdims=False)
        send = lax.dynamic_index_in_dim(blocks, 1 - mine, axis=where, keepdims=False)
        pairs = [(i, i ^ (1 << b)) for i in range(peers)]
        got = lax.ppermute(send, axis, pairs)
        blocks = keep + got
    return blocks


def source_plane(rows_x, rows_y, amounts, width_x, width_y):
    onehot_x = (rows_x[:, None] == jnp.arange(width_x, dtype=jnp.int32)[None, :]).astype(
        jnp.float32
    )
    onehot_y = (rows_y[:, None] == jnp.arange(width_y, dtype=jnp.int32)[None, :]).astype(
        jnp.float32
    )
    return jnp.dot((onehot_x * amounts[:, None]).T, onehot_y, precision=lax.Precision.HIGHEST)


def split_halo(shard, width):
    depth, shots = lax.axis_size("depth"), lax.axis_size("shots")
    core = lax.axis_index("shots") % 2
    length = shard.shape[1]
    start = jnp.where(core == 0, length - width, 0)
    sent = lax.dynamic_slice_in_dim(shard, start, width, axis=1)
    pairs = []
    for d in range(depth):
        for s in range(shots):
            to = d + 1 if s % 2 == 0 else d - 1
            if 0 <= to < depth:
                pairs.append((d * shots + s, to * shots + s))
    got = lax.ppermute(sent, ("depth", "shots"), pairs)
    other = lax.ppermute(got, "shots", [(s, s ^ 1) for s in range(shots)])
    return got, other


def body(adj_now, adj_prev, fwd_snap, velocity, density, shot_count, rec_x, rec_y, residual):
    width_x = adj_now.shape[2]
    width_y = adj_now.shape[3]
    steps = fwd_snap.shape[1]
    groups = lax.axis_size("shots")
    adj_lo, adj_hi = halo_of(jnp.stack([adj_now[0], adj_prev[0]]), "depth", 1, HALO)
    local = jnp.stack([density * velocity * velocity, 1.0 / density])
    packed = gather_rows(local, "shots", 2)
    mat_lo, mat_hi = split_halo(packed, HALO)
    holds_source = (lax.axis_index("depth") == 0).astype(jnp.float32)
    src = jnp.stack(
        [source_plane(rec_x[0], rec_y[0], residual[0, t], width_x, width_y) for t in range(steps)]
    ) * holds_source
    core = (lax.axis_index("shots") % 2).astype(jnp.float32)
    count = jnp.concatenate([shot_count.astype(jnp.float32), core[None]])
    current, older, weighted = run_steps(
        count, adj_now[0], adj_prev[0], adj_lo, adj_hi, packed, mat_lo, mat_hi, fwd_snap[0], src
    )
    summed = scatter_rows(weighted, "shots", 1)
    grad_vel = 2.0 * density * velocity * summed / (4.0 * groups)
    return (current[None], older[None], grad_vel)


def solution(mesh):
    in_specs = (
        P("shots", "depth", None, None),
        P("shots", "depth", None, None),
        P("shots", None, "depth", None, None),
        P("depth", "shots", None),
        P("depth", "shots", None),
        P("shots"),
        P("shots", None),
        P("shots", None),
        P("shots", None, None),
    )
    out_specs = (
        P("shots", "depth", None, None),
        P("shots", "depth", None, None),
        P("depth", "shots", None),
    )
    return jax.shard_map(body, mesh=mesh, in_specs=in_specs, out_specs=out_specs, check_vma=False)
```

```python
import jax
import jax.numpy as jnp
from jax import lax
from jax.sharding import PartitionSpec as P
from jax.experimental import pallas as pl
from jax.experimental.pallas import tpu as pltpu

INTERPRET = False

HALO = 4


def shift_fwd(v, axis, n):
    r = pltpu.roll(v, n - 1, axis)
    idx = lax.broadcasted_iota(jnp.int32, v.shape, axis)
    return jnp.where(idx == n - 1, 0.0, r)


def shift_bwd(v, axis):
    r = pltpu.roll(v, 1, axis)
    idx = lax.broadcasted_iota(jnp.int32, v.shape, axis)
    return jnp.where(idx == 0, 0.0, r)


def stencil_kernel(count_ref, now_hbm, prev_hbm, adj_lo, adj_hi, mat_hbm, mat_lo, mat_hi, snap_hbm,
                   src_hbm, now_ref, prev_ref, img_ref, curb, oldb, matb, snapb, srcb, pbuf, qbuf,
                   kz, kxf, kxb, kyf, kyb, kk, sems):
    ext = curb.shape[0]
    nx, ny = curb.shape[1], curb.shape[2]
    planes = ext - 2 * HALO
    steps = snapb.shape[0]
    count = count_ref[0]
    copies = []

    def fetch(src, dst):
        c = pltpu.make_async_copy(src, dst, sems.at[len(copies)])
        c.start()
        copies.append(c)
        return c

    inner_at, lo_at, hi_at = pl.ds(HALO, planes), pl.ds(0, HALO), pl.ds(HALO + planes, HALO)
    need_mat = [fetch(mat_hbm, matb.at[:, inner_at])]
    own = pltpu.make_async_copy(mat_lo, matb.at[:, lo_at], sems.at[10 + steps])
    swapped = pltpu.make_async_copy(mat_hi, matb.at[:, hi_at], sems.at[11 + steps])

    @pl.when(count_ref[1] == 0.0)
    def _():
        own.start()
        swapped.start()

    @pl.when(count_ref[1] != 0.0)
    def _():
        pltpu.make_async_copy(mat_lo, matb.at[:, hi_at], sems.at[11 + steps]).start()
        pltpu.make_async_copy(mat_hi, matb.at[:, lo_at], sems.at[10 + steps]).start()

    need_mat += [own, swapped]
    need_adj = [fetch(now_hbm, curb.at[inner_at]), fetch(adj_lo.at[0], curb.at[lo_at]),
                fetch(adj_hi.at[0], curb.at[hi_at]), fetch(prev_hbm, oldb.at[inner_at]),
                fetch(adj_lo.at[1], oldb.at[lo_at]), fetch(adj_hi.at[1], oldb.at[hi_at]),
                fetch(src_hbm, srcb)]
    need_snap = [fetch(snap_hbm.at[steps - 1 - step], snapb.at[steps - 1 - step])
                 for step in range(steps)]
    for c in need_mat:
        c.wait()

    def weights(e, carry):
        bc = matb[1, e]
        kz[e] = 0.5 * (bc + matb[1, e + 1])
        kxf[e] = 0.5 * (bc + shift_fwd(bc, 0, nx))
        kxb[e] = 0.5 * (shift_bwd(bc, 0) + bc)
        kyf[e] = 0.5 * (bc + shift_fwd(bc, 1, ny))
        kyb[e] = 0.5 * (shift_bwd(bc, 1) + bc)
        kk[e] = 0.08 * matb[0, e]
        return carry

    lax.fori_loop(0, ext - 1, weights, 0)
    for c in need_adj:
        c.wait()

    def one_step(step, cur, old, dst, lo, hi):
        moment = steps - 1 - step
        need_snap[step].wait()

        def plane(e, with_source):
            pc = cur(e)
            total = kz[e] * (cur(e + 1) - pc) - kz[e - 1] * (pc - cur(e - 1))
            total = total + (kxf[e] * (shift_fwd(pc, 0, nx) - pc) - kxb[e] * (pc - shift_bwd(pc, 0)))
            total = total + (kyf[e] * (shift_fwd(pc, 1, ny) - pc) - kyb[e] * (pc - shift_bwd(pc, 1)))
            new = 2.0 * pc - old(e) + kk[e] * total
            if with_source:
                new = new + 0.08 * srcb[moment]
            dst(e, new)
            inner = jnp.logical_and(e >= HALO, e < ext - HALO)

            @pl.when(inner)
            def _():
                z = e - HALO
                gained = snapb[moment, z].astype(jnp.float32) * new
                if step == 0:
                    img_ref[z] = gained
                elif step == steps - 1:
                    img_ref[z] = count * (img_ref[z] + gained)
                else:
                    img_ref[z] = img_ref[z] + gained

        def plain(e, carry):
            plane(e, False)
            return carry

        at_source = HALO + 2
        lax.fori_loop(lo, at_source, plain, 0)
        plane(at_source, True)
        lax.fori_loop(at_source + 1, hi, plain, 0, unroll=2)

    def rd(ref):
        return lambda e: ref[e]

    def wr(ref):
        def f(e, v):
            ref[e] = v

        return f

    def wr_inner(ref, out):
        def f(e, v):
            ref[e] = v

            @pl.when(jnp.logical_and(e >= HALO, e < ext - HALO))
            def _():
                out[e - HALO] = v

        return f

    def wr_out(out):
        def f(e, v):
            out[e - HALO] = v

        return f

    one_step(0, rd(curb), rd(oldb), wr(pbuf), 1, ext - 1)
    one_step(1, rd(pbuf), rd(curb), wr(qbuf), 2, ext - 2)
    one_step(2, rd(qbuf), rd(pbuf), wr_inner(pbuf, prev_ref), 3, ext - 3)
    one_step(3, rd(pbuf), rd(qbuf), wr_out(now_ref), HALO, ext - HALO)


def run_steps(count, adj_now, adj_prev, adj_lo, adj_hi, mat, mat_lo, mat_hi, snaps, src):
    planes, nx, ny = adj_now.shape
    ext = planes + 2 * HALO
    steps = snaps.shape[0]
    vmem = pltpu.VMEM
    out_shape = [jax.ShapeDtypeStruct((planes, nx, ny), jnp.float32)] * 3
    field = pltpu.VMEM((ext, nx, ny), jnp.float32)
    return pl.pallas_call(
        stencil_kernel,
        out_shape=out_shape,
        in_specs=[pl.BlockSpec(memory_space=pltpu.SMEM)] + [pl.BlockSpec(memory_space=pl.ANY)] * 9,
        out_specs=[pl.BlockSpec(memory_space=vmem)] * 3,
        scratch_shapes=[field, field, pltpu.VMEM((2, ext, nx, ny), jnp.float32),
                        pltpu.VMEM(snaps.shape, snaps.dtype), pltpu.VMEM(src.shape, jnp.float32)]
        + [field] * 8 + [pltpu.SemaphoreType.DMA((12 + steps,))],
        compiler_params=pltpu.CompilerParams(vmem_limit_bytes=56 * 1024 * 1024),
        interpret=INTERPRET,
    )(count, adj_now, adj_prev, adj_lo, adj_hi, mat, mat_lo, mat_hi, snaps, src)


def halo_of(shard, axis, dim, width):
    peers, length = (lax.axis_size(axis), shard.shape[dim])
    up = [(i, (i + 1) % peers) for i in range(peers - 1)]
    down = [(j, i) for i, j in up]
    last = lax.slice_in_dim(shard, length - width, length, axis=dim)
    first = lax.slice_in_dim(shard, 0, width, axis=dim)
    return lax.ppermute(last, axis, up), lax.ppermute(first, axis, down)


def bit_order(peers):
    return list(range(peers.bit_length() - 1))


def gather_rows(shard, axis, dim):
    peers = lax.axis_size(axis)
    me = lax.axis_index(axis)
    pieces = jnp.expand_dims(shard, dim)
    for b in reversed(bit_order(peers)):
        pairs = [(i, i ^ (1 << b)) for i in range(peers)]
        got = lax.ppermute(pieces, axis, pairs)
        mine = (me >> b) & 1
        lo = jnp.where(mine == 0, pieces, got)
        hi = jnp.where(mine == 0, got, pieces)
        both = jnp.stack([lo, hi], axis=dim + 1)
        shape = list(pieces.shape)
        shape[dim] = shape[dim] * 2
        pieces = both.reshape(shape)
    shape = list(shard.shape)
    shape[dim] = shape[dim] * peers
    return pieces.reshape(shape)


def scatter_rows(full, axis, dim):
    peers = lax.axis_size(axis)
    me = lax.axis_index(axis)
    nbits = peers.bit_length() - 1
    rows = full.shape[dim] // peers
    shape = list(full.shape)
    blocks = full.reshape(shape[:dim] + [2] * nbits + [rows] + shape[dim + 1:])
    for b in bit_order(peers):
        where = dim + (nbits - 1 - b)
        mine = (me >> b) & 1
        keep = lax.dynamic_index_in_dim(blocks, mine, axis=where, keepdims=False)
        send = lax.dynamic_index_in_dim(blocks, 1 - mine, axis=where, keepdims=False)
        pairs = [(i, i ^ (1 << b)) for i in range(peers)]
        got = lax.ppermute(send, axis, pairs)
        blocks = keep + got
    return blocks


def source_plane(rows_x, rows_y, amounts, width_x, width_y):
    onehot_x = (rows_x[:, None] == jnp.arange(width_x, dtype=jnp.int32)[None, :]).astype(
        jnp.float32
    )
    onehot_y = (rows_y[:, None] == jnp.arange(width_y, dtype=jnp.int32)[None, :]).astype(
        jnp.float32
    )
    return jnp.dot((onehot_x * amounts[:, None]).T, onehot_y, precision=lax.Precision.HIGHEST)


def split_halo(shard, width):
    depth, shots = lax.axis_size("depth"), lax.axis_size("shots")
    core = lax.axis_index("shots") % 2
    length = shard.shape[1]
    start = jnp.where(core == 0, length - width, 0)
    sent = lax.dynamic_slice_in_dim(shard, start, width, axis=1)
    pairs = []
    for d in range(depth):
        for s in range(shots):
            to = d + 1 if s % 2 == 0 else d - 1
            if 0 <= to < depth:
                pairs.append((d * shots + s, to * shots + s))
    got = lax.ppermute(sent, ("depth", "shots"), pairs)
    other = lax.ppermute(got, "shots", [(s, s ^ 1) for s in range(shots)])
    return got, other


def body(adj_now, adj_prev, fwd_snap, velocity, density, shot_count, rec_x, rec_y, residual):
    width_x = adj_now.shape[2]
    width_y = adj_now.shape[3]
    steps = fwd_snap.shape[1]
    groups = lax.axis_size("shots")
    adj_lo, adj_hi = halo_of(jnp.stack([adj_now[0], adj_prev[0]]), "depth", 1, HALO)
    local = jnp.stack([density * velocity * velocity, 1.0 / density])
    packed = gather_rows(local, "shots", 2)
    mat_lo, mat_hi = split_halo(packed, HALO)
    holds_source = (lax.axis_index("depth") == 0).astype(jnp.float32)
    src = jnp.stack(
        [source_plane(rec_x[0], rec_y[0], residual[0, t], width_x, width_y) for t in range(steps)]
    ) * holds_source
    core = (lax.axis_index("shots") % 2).astype(jnp.float32)
    count = jnp.concatenate([shot_count.astype(jnp.float32), core[None]])
    current, older, weighted = run_steps(
        count, adj_now[0], adj_prev[0], adj_lo, adj_hi, packed, mat_lo, mat_hi, fwd_snap[0], src
    )
    summed = scatter_rows(weighted, "shots", 1)
    grad_vel = 2.0 * density * velocity * summed / (4.0 * groups)
    return (current[None], older[None], grad_vel)


def solution(mesh):
    in_specs = (
        P("shots", "depth", None, None),
        P("shots", "depth", None, None),
        P("shots", None, "depth", None, None),
        P("depth", "shots", None),
        P("depth", "shots", None),
        P("shots"),
        P("shots", None),
        P("shots", None),
        P("shots", None, None),
    )
    out_specs = (
        P("shots", "depth", None, None),
        P("shots", "depth", None, None),
        P("depth", "shots", None),
    )
    return jax.shard_map(body, mesh=mesh, in_specs=in_specs, out_specs=out_specs, check_vma=False)
```

```python
import jax
import jax.numpy as jnp
from jax import lax
from jax.sharding import PartitionSpec as P
from jax.experimental import pallas as pl
from jax.experimental.pallas import tpu as pltpu

INTERPRET = False

HALO = 4


def shift_fwd(v, axis, n):
    r = pltpu.roll(v, n - 1, axis)
    idx = lax.broadcasted_iota(jnp.int32, v.shape, axis)
    return jnp.where(idx == n - 1, 0.0, r)


def shift_bwd(v, axis):
    r = pltpu.roll(v, 1, axis)
    idx = lax.broadcasted_iota(jnp.int32, v.shape, axis)
    return jnp.where(idx == 0, 0.0, r)


def stencil_kernel(count_ref, now_hbm, prev_hbm, adj_lo, adj_hi, mat_hbm, mat_lo, mat_hi, snap_hbm,
                   src_hbm, now_ref, prev_ref, img_ref, curb, oldb, matb, snapb, srcb, pbuf, qbuf,
                   kz, kxf, kxb, kyf, kyb, kk, sems):
    ext = curb.shape[0]
    nx, ny = curb.shape[1], curb.shape[2]
    planes = ext - 2 * HALO
    steps = snapb.shape[0]
    count = count_ref[0]
    copies = []

    def fetch(src, dst):
        c = pltpu.make_async_copy(src, dst, sems.at[len(copies)])
        c.start()
        copies.append(c)
        return c

    inner_at, lo_at, hi_at = pl.ds(HALO, planes), pl.ds(0, HALO), pl.ds(HALO + planes, HALO)
    need_mat = [fetch(mat_hbm, matb.at[:, inner_at])]
    own = pltpu.make_async_copy(mat_lo, matb.at[:, lo_at], sems.at[10 + steps])
    swapped = pltpu.make_async_copy(mat_hi, matb.at[:, hi_at], sems.at[11 + steps])

    @pl.when(count_ref[1] == 0.0)
    def _():
        own.start()
        swapped.start()

    @pl.when(count_ref[1] != 0.0)
    def _():
        pltpu.make_async_copy(mat_lo, matb.at[:, hi_at], sems.at[11 + steps]).start()
        pltpu.make_async_copy(mat_hi, matb.at[:, lo_at], sems.at[10 + steps]).start()

    need_mat += [own, swapped]
    need_adj = [fetch(now_hbm, curb.at[inner_at]), fetch(adj_lo.at[0], curb.at[lo_at]),
                fetch(adj_hi.at[0], curb.at[hi_at]), fetch(prev_hbm, oldb.at[inner_at]),
                fetch(adj_lo.at[1], oldb.at[lo_at]), fetch(adj_hi.at[1], oldb.at[hi_at]),
                fetch(src_hbm, srcb)]
    need_snap = [fetch(snap_hbm.at[steps - 1 - step], snapb.at[steps - 1 - step])
                 for step in range(steps)]
    for c in need_mat:
        c.wait()

    def weights(e, carry):
        bc = matb[1, e]
        kz[e] = 0.5 * (bc + matb[1, e + 1])
        kxf[e] = 0.5 * (bc + shift_fwd(bc, 0, nx))
        kxb[e] = 0.5 * (shift_bwd(bc, 0) + bc)
        kyf[e] = 0.5 * (bc + shift_fwd(bc, 1, ny))
        kyb[e] = 0.5 * (shift_bwd(bc, 1) + bc)
        kk[e] = 0.08 * matb[0, e]
        return carry

    lax.fori_loop(0, ext - 1, weights, 0)
    for c in need_adj:
        c.wait()

    def one_step(step, cur, old, dst, lo, hi):
        moment = steps - 1 - step
        need_snap[step].wait()

        def plane(e, with_source):
            pc = cur(e)
            total = kz[e] * (cur(e + 1) - pc) - kz[e - 1] * (pc - cur(e - 1))
            total = total + (kxf[e] * (shift_fwd(pc, 0, nx) - pc) - kxb[e] * (pc - shift_bwd(pc, 0)))
            total = total + (kyf[e] * (shift_fwd(pc, 1, ny) - pc) - kyb[e] * (pc - shift_bwd(pc, 1)))
            new = 2.0 * pc - old(e) + kk[e] * total
            if with_source:
                new = new + 0.08 * srcb[moment]
            dst(e, new)
            inner = jnp.logical_and(e >= HALO, e < ext - HALO)

            @pl.when(inner)
            def _():
                z = e - HALO
                gained = snapb[moment, z].astype(jnp.float32) * new
                if step == 0:
                    img_ref[z] = gained
                elif step == steps - 1:
                    img_ref[z] = count * (img_ref[z] + gained)
                else:
                    img_ref[z] = img_ref[z] + gained

        def plain(e, carry):
            plane(e, False)
            return carry

        at_source = HALO + 2
        lax.fori_loop(lo, at_source, plain, 0)
        plane(at_source, True)
        lax.fori_loop(at_source + 1, hi, plain, 0, unroll=2)

    def rd(ref):
        return lambda e: ref[e]

    def wr(ref):
        def f(e, v):
            ref[e] = v

        return f

    def wr_out(out):
        def f(e, v):
            out[e - HALO] = v

        return f

    one_step(0, rd(curb), rd(oldb), wr(pbuf), 1, ext - 1)
    one_step(1, rd(pbuf), rd(curb), wr(qbuf), 2, ext - 2)
    one_step(2, rd(qbuf), rd(pbuf), wr(pbuf), 3, ext - 3)
    put_prev = pltpu.make_async_copy(pbuf.at[inner_at], prev_ref, sems.at[12])
    put_prev.start()
    one_step(3, rd(pbuf), rd(qbuf), wr_out(now_ref), HALO, ext - HALO)
    put_prev.wait()


def run_steps(count, adj_now, adj_prev, adj_lo, adj_hi, mat, mat_lo, mat_hi, snaps, src):
    planes, nx, ny = adj_now.shape
    ext = planes + 2 * HALO
    steps = snaps.shape[0]
    vmem = pltpu.VMEM
    out_shape = [jax.ShapeDtypeStruct((planes, nx, ny), jnp.float32)] * 3
    field = pltpu.VMEM((ext, nx, ny), jnp.float32)
    return pl.pallas_call(
        stencil_kernel,
        out_shape=out_shape,
        in_specs=[pl.BlockSpec(memory_space=pltpu.SMEM)] + [pl.BlockSpec(memory_space=pl.ANY)] * 9,
        out_specs=[pl.BlockSpec(memory_space=vmem), pl.BlockSpec(memory_space=pl.ANY),
                   pl.BlockSpec(memory_space=vmem)],
        scratch_shapes=[field, field, pltpu.VMEM((2, ext, nx, ny), jnp.float32),
                        pltpu.VMEM(snaps.shape, snaps.dtype), pltpu.VMEM(src.shape, jnp.float32)]
        + [field] * 8 + [pltpu.SemaphoreType.DMA((12 + steps,))],
        compiler_params=pltpu.CompilerParams(vmem_limit_bytes=56 * 1024 * 1024),
        interpret=INTERPRET,
    )(count, adj_now, adj_prev, adj_lo, adj_hi, mat, mat_lo, mat_hi, snaps, src)


def halo_of(shard, axis, dim, width):
    peers, length = (lax.axis_size(axis), shard.shape[dim])
    up = [(i, (i + 1) % peers) for i in range(peers - 1)]
    down = [(j, i) for i, j in up]
    last = lax.slice_in_dim(shard, length - width, length, axis=dim)
    first = lax.slice_in_dim(shard, 0, width, axis=dim)
    return lax.ppermute(last, axis, up), lax.ppermute(first, axis, down)


def bit_order(peers):
    return list(range(peers.bit_length() - 1))


def gather_rows(shard, axis, dim):
    peers = lax.axis_size(axis)
    me = lax.axis_index(axis)
    pieces = jnp.expand_dims(shard, dim)
    for b in reversed(bit_order(peers)):
        pairs = [(i, i ^ (1 << b)) for i in range(peers)]
        got = lax.ppermute(pieces, axis, pairs)
        mine = (me >> b) & 1
        lo = jnp.where(mine == 0, pieces, got)
        hi = jnp.where(mine == 0, got, pieces)
        both = jnp.stack([lo, hi], axis=dim + 1)
        shape = list(pieces.shape)
        shape[dim] = shape[dim] * 2
        pieces = both.reshape(shape)
    shape = list(shard.shape)
    shape[dim] = shape[dim] * peers
    return pieces.reshape(shape)


def scatter_rows(full, axis, dim):
    peers = lax.axis_size(axis)
    me = lax.axis_index(axis)
    nbits = peers.bit_length() - 1
    rows = full.shape[dim] // peers
    shape = list(full.shape)
    blocks = full.reshape(shape[:dim] + [2] * nbits + [rows] + shape[dim + 1:])
    for b in bit_order(peers):
        where = dim + (nbits - 1 - b)
        mine = (me >> b) & 1
        keep = lax.dynamic_index_in_dim(blocks, mine, axis=where, keepdims=False)
        send = lax.dynamic_index_in_dim(blocks, 1 - mine, axis=where, keepdims=False)
        pairs = [(i, i ^ (1 << b)) for i in range(peers)]
        got = lax.ppermute(send, axis, pairs)
        blocks = keep + got
    return blocks


def source_plane(rows_x, rows_y, amounts, width_x, width_y):
    onehot_x = (rows_x[:, None] == jnp.arange(width_x, dtype=jnp.int32)[None, :]).astype(
        jnp.float32
    )
    onehot_y = (rows_y[:, None] == jnp.arange(width_y, dtype=jnp.int32)[None, :]).astype(
        jnp.float32
    )
    return jnp.dot((onehot_x * amounts[:, None]).T, onehot_y, precision=lax.Precision.HIGHEST)


def split_halo(shard, width):
    depth, shots = lax.axis_size("depth"), lax.axis_size("shots")
    core = lax.axis_index("shots") % 2
    length = shard.shape[1]
    start = jnp.where(core == 0, length - width, 0)
    sent = lax.dynamic_slice_in_dim(shard, start, width, axis=1)
    pairs = []
    for d in range(depth):
        for s in range(shots):
            to = d + 1 if s % 2 == 0 else d - 1
            if 0 <= to < depth:
                pairs.append((d * shots + s, to * shots + s))
    got = lax.ppermute(sent, ("depth", "shots"), pairs)
    other = lax.ppermute(got, "shots", [(s, s ^ 1) for s in range(shots)])
    return got, other


def body(adj_now, adj_prev, fwd_snap, velocity, density, shot_count, rec_x, rec_y, residual):
    width_x = adj_now.shape[2]
    width_y = adj_now.shape[3]
    steps = fwd_snap.shape[1]
    groups = lax.axis_size("shots")
    adj_lo, adj_hi = halo_of(jnp.stack([adj_now[0], adj_prev[0]]), "depth", 1, HALO)
    local = jnp.stack([density * velocity * velocity, 1.0 / density])
    packed = gather_rows(local, "shots", 2)
    mat_lo, mat_hi = split_halo(packed, HALO)
    holds_source = (lax.axis_index("depth") == 0).astype(jnp.float32)
    src = jnp.stack(
        [source_plane(rec_x[0], rec_y[0], residual[0, t], width_x, width_y) for t in range(steps)]
    ) * holds_source
    core = (lax.axis_index("shots") % 2).astype(jnp.float32)
    count = jnp.concatenate([shot_count.astype(jnp.float32), core[None]])
    current, older, weighted = run_steps(
        count, adj_now[0], adj_prev[0], adj_lo, adj_hi, packed, mat_lo, mat_hi, fwd_snap[0], src
    )
    summed = scatter_rows(weighted, "shots", 1)
    grad_vel = 2.0 * density * velocity * summed / (4.0 * groups)
    return (current[None], older[None], grad_vel)


def solution(mesh):
    in_specs = (
        P("shots", "depth", None, None),
        P("shots", "depth", None, None),
        P("shots", None, "depth", None, None),
        P("depth", "shots", None),
        P("depth", "shots", None),
        P("shots"),
        P("shots", None),
        P("shots", None),
        P("shots", None, None),
    )
    out_specs = (
        P("shots", "depth", None, None),
        P("shots", "depth", None, None),
        P("depth", "shots", None),
    )
    return jax.shard_map(body, mesh=mesh, in_specs=in_specs, out_specs=out_specs, check_vma=False)
```

```python
import jax
import jax.numpy as jnp
from jax import lax
from jax.sharding import PartitionSpec as P
from jax.experimental import pallas as pl
from jax.experimental.pallas import tpu as pltpu

INTERPRET = False

HALO = 4


def shift_fwd(v, axis, n):
    r = pltpu.roll(v, n - 1, axis)
    idx = lax.broadcasted_iota(jnp.int32, v.shape, axis)
    return jnp.where(idx == n - 1, 0.0, r)


def shift_bwd(v, axis):
    r = pltpu.roll(v, 1, axis)
    idx = lax.broadcasted_iota(jnp.int32, v.shape, axis)
    return jnp.where(idx == 0, 0.0, r)


def stencil_kernel(count_ref, now_hbm, prev_hbm, adj_lo, adj_hi, mat_hbm, mat_lo, mat_hi, snap_hbm,
                   src_hbm, now_ref, prev_ref, img_ref, curb, oldb, matb, snapb, srcb, pbuf, qbuf,
                   kz, kxf, kxb, kyf, kyb, kk, sems):
    ext = curb.shape[0]
    nx, ny = curb.shape[1], curb.shape[2]
    planes = ext - 2 * HALO
    steps = snapb.shape[0]
    count = count_ref[0]
    copies = []

    def fetch(src, dst):
        c = pltpu.make_async_copy(src, dst, sems.at[len(copies)])
        c.start()
        copies.append(c)
        return c

    inner_at, lo_at, hi_at = pl.ds(HALO, planes), pl.ds(0, HALO), pl.ds(HALO + planes, HALO)
    need_mat = [fetch(mat_hbm, matb.at[:, inner_at])]

    def place(below, above):
        return [
            pltpu.make_async_copy(below.at[pl.ds(0, HALO)], matb.at[1, pl.ds(0, HALO)], sems.at[14]),
            pltpu.make_async_copy(below.at[pl.ds(HALO, HALO - 1)], matb.at[0, pl.ds(1, HALO - 1)],
                                  sems.at[15]),
            pltpu.make_async_copy(above.at[pl.ds(0, HALO)], matb.at[1, pl.ds(HALO + planes, HALO)],
                                  sems.at[16]),
            pltpu.make_async_copy(above.at[pl.ds(HALO, HALO - 1)],
                                  matb.at[0, pl.ds(HALO + planes, HALO - 1)], sems.at[17]),
        ]

    own = place(mat_lo, mat_hi)
    swapped = place(mat_hi, mat_lo)

    @pl.when(count_ref[1] == 0.0)
    def _():
        for c in own:
            c.start()

    @pl.when(count_ref[1] != 0.0)
    def _():
        for c in swapped:
            c.start()

    need_mat += own
    need_adj = [fetch(now_hbm, curb.at[inner_at]), fetch(adj_lo.at[0], curb.at[lo_at]),
                fetch(adj_hi.at[0], curb.at[hi_at]), fetch(prev_hbm, oldb.at[inner_at]),
                fetch(adj_lo.at[1], oldb.at[lo_at]), fetch(adj_hi.at[1], oldb.at[hi_at]),
                fetch(src_hbm, srcb)]
    need_snap = [fetch(snap_hbm.at[steps - 1 - step], snapb.at[steps - 1 - step])
                 for step in range(steps)]
    for c in need_mat:
        c.wait()

    def weights(e, carry):
        bc = matb[1, e]
        kz[e] = 0.5 * (bc + matb[1, e + 1])
        kxf[e] = 0.5 * (bc + shift_fwd(bc, 0, nx))
        kxb[e] = 0.5 * (shift_bwd(bc, 0) + bc)
        kyf[e] = 0.5 * (bc + shift_fwd(bc, 1, ny))
        kyb[e] = 0.5 * (shift_bwd(bc, 1) + bc)
        kk[e] = 0.08 * matb[0, e]
        return carry

    lax.fori_loop(0, ext - 1, weights, 0)
    for c in need_adj:
        c.wait()

    def one_step(step, cur, old, dst, lo, hi):
        moment = steps - 1 - step
        need_snap[step].wait()

        def plane(e, with_source):
            pc = cur(e)
            total = kz[e] * (cur(e + 1) - pc) - kz[e - 1] * (pc - cur(e - 1))
            total = total + (kxf[e] * (shift_fwd(pc, 0, nx) - pc) - kxb[e] * (pc - shift_bwd(pc, 0)))
            total = total + (kyf[e] * (shift_fwd(pc, 1, ny) - pc) - kyb[e] * (pc - shift_bwd(pc, 1)))
            new = 2.0 * pc - old(e) + kk[e] * total
            if with_source:
                new = new + 0.08 * srcb[moment]
            dst(e, new)
            inner = jnp.logical_and(e >= HALO, e < ext - HALO)

            @pl.when(inner)
            def _():
                z = e - HALO
                gained = snapb[moment, z].astype(jnp.float32) * new
                if step == 0:
                    img_ref[z] = gained
                elif step == steps - 1:
                    img_ref[z] = count * (img_ref[z] + gained)
                else:
                    img_ref[z] = img_ref[z] + gained

        def plain(e, carry):
            plane(e, False)
            return carry

        at_source = HALO + 2
        lax.fori_loop(lo, at_source, plain, 0)
        plane(at_source, True)
        lax.fori_loop(at_source + 1, hi, plain, 0, unroll=2)

    def rd(ref):
        return lambda e: ref[e]

    def wr(ref):
        def f(e, v):
            ref[e] = v

        return f

    def wr_out(out):
        def f(e, v):
            out[e - HALO] = v

        return f

    one_step(0, rd(curb), rd(oldb), wr(pbuf), 1, ext - 1)
    one_step(1, rd(pbuf), rd(curb), wr(qbuf), 2, ext - 2)
    one_step(2, rd(qbuf), rd(pbuf), wr(pbuf), 3, ext - 3)
    put_prev = pltpu.make_async_copy(pbuf.at[inner_at], prev_ref, sems.at[12])
    put_prev.start()
    one_step(3, rd(pbuf), rd(qbuf), wr_out(now_ref), HALO, ext - HALO)
    put_prev.wait()


def run_steps(count, adj_now, adj_prev, adj_lo, adj_hi, mat, mat_lo, mat_hi, snaps, src):
    planes, nx, ny = adj_now.shape
    ext = planes + 2 * HALO
    steps = snaps.shape[0]
    vmem = pltpu.VMEM
    out_shape = [jax.ShapeDtypeStruct((planes, nx, ny), jnp.float32)] * 3
    field = pltpu.VMEM((ext, nx, ny), jnp.float32)
    return pl.pallas_call(
        stencil_kernel,
        out_shape=out_shape,
        in_specs=[pl.BlockSpec(memory_space=pltpu.SMEM)] + [pl.BlockSpec(memory_space=pl.ANY)] * 9,
        out_specs=[pl.BlockSpec(memory_space=vmem), pl.BlockSpec(memory_space=pl.ANY),
                   pl.BlockSpec(memory_space=vmem)],
        scratch_shapes=[field, field, pltpu.VMEM((2, ext, nx, ny), jnp.float32),
                        pltpu.VMEM(snaps.shape, snaps.dtype), pltpu.VMEM(src.shape, jnp.float32)]
        + [field] * 8 + [pltpu.SemaphoreType.DMA((14 + steps,))],
        compiler_params=pltpu.CompilerParams(vmem_limit_bytes=56 * 1024 * 1024),
        interpret=INTERPRET,
    )(count, adj_now, adj_prev, adj_lo, adj_hi, mat, mat_lo, mat_hi, snaps, src)


def halo_of(shard, axis, dim, width):
    peers, length = (lax.axis_size(axis), shard.shape[dim])
    up = [(i, (i + 1) % peers) for i in range(peers - 1)]
    down = [(j, i) for i, j in up]
    last = lax.slice_in_dim(shard, length - width, length, axis=dim)
    first = lax.slice_in_dim(shard, 0, width, axis=dim)
    return lax.ppermute(last, axis, up), lax.ppermute(first, axis, down)


def bit_order(peers):
    return list(range(peers.bit_length() - 1))


def gather_rows(shard, axis, dim):
    peers = lax.axis_size(axis)
    me = lax.axis_index(axis)
    pieces = jnp.expand_dims(shard, dim)
    for b in reversed(bit_order(peers)):
        pairs = [(i, i ^ (1 << b)) for i in range(peers)]
        got = lax.ppermute(pieces, axis, pairs)
        mine = (me >> b) & 1
        lo = jnp.where(mine == 0, pieces, got)
        hi = jnp.where(mine == 0, got, pieces)
        both = jnp.stack([lo, hi], axis=dim + 1)
        shape = list(pieces.shape)
        shape[dim] = shape[dim] * 2
        pieces = both.reshape(shape)
    shape = list(shard.shape)
    shape[dim] = shape[dim] * peers
    return pieces.reshape(shape)


def scatter_rows(full, axis, dim):
    peers = lax.axis_size(axis)
    me = lax.axis_index(axis)
    nbits = peers.bit_length() - 1
    rows = full.shape[dim] // peers
    shape = list(full.shape)
    blocks = full.reshape(shape[:dim] + [2] * nbits + [rows] + shape[dim + 1:])
    for b in bit_order(peers):
        where = dim + (nbits - 1 - b)
        mine = (me >> b) & 1
        keep = lax.dynamic_index_in_dim(blocks, mine, axis=where, keepdims=False)
        send = lax.dynamic_index_in_dim(blocks, 1 - mine, axis=where, keepdims=False)
        pairs = [(i, i ^ (1 << b)) for i in range(peers)]
        got = lax.ppermute(send, axis, pairs)
        blocks = keep + got
    return blocks


def source_plane(rows_x, rows_y, amounts, width_x, width_y):
    onehot_x = (rows_x[:, None] == jnp.arange(width_x, dtype=jnp.int32)[None, :]).astype(
        jnp.float32
    )
    onehot_y = (rows_y[:, None] == jnp.arange(width_y, dtype=jnp.int32)[None, :]).astype(
        jnp.float32
    )
    return jnp.dot((onehot_x * amounts[:, None]).T, onehot_y, precision=lax.Precision.HIGHEST)


def split_halo(shard, width):
    depth, shots = lax.axis_size("depth"), lax.axis_size("shots")
    core = lax.axis_index("shots") % 2
    length = shard.shape[1]
    buoy = lax.dynamic_slice_in_dim(shard[1], jnp.where(core == 0, length - width, 0), width, 0)
    kappa = lax.dynamic_slice_in_dim(shard[0], jnp.where(core == 0, length - width + 1, 0), width - 1, 0)
    sent = jnp.concatenate([buoy, kappa])
    pairs = []
    for d in range(depth):
        for s in range(shots):
            to = d + 1 if s % 2 == 0 else d - 1
            if 0 <= to < depth:
                pairs.append((d * shots + s, to * shots + s))
    got = lax.ppermute(sent, ("depth", "shots"), pairs)
    other = lax.ppermute(got, "shots", [(s, s ^ 1) for s in range(shots)])
    return got, other


def body(adj_now, adj_prev, fwd_snap, velocity, density, shot_count, rec_x, rec_y, residual):
    width_x = adj_now.shape[2]
    width_y = adj_now.shape[3]
    steps = fwd_snap.shape[1]
    groups = lax.axis_size("shots")
    adj_lo, adj_hi = halo_of(jnp.stack([adj_now[0], adj_prev[0]]), "depth", 1, HALO)
    local = jnp.stack([density * velocity * velocity, 1.0 / density])
    packed = gather_rows(local, "shots", 2)
    mat_lo, mat_hi = split_halo(packed, HALO)
    holds_source = (lax.axis_index("depth") == 0).astype(jnp.float32)
    src = jnp.stack(
        [source_plane(rec_x[0], rec_y[0], residual[0, t], width_x, width_y) for t in range(steps)]
    ) * holds_source
    core = (lax.axis_index("shots") % 2).astype(jnp.float32)
    count = jnp.concatenate([shot_count.astype(jnp.float32), core[None]])
    current, older, weighted = run_steps(
        count, adj_now[0], adj_prev[0], adj_lo, adj_hi, packed, mat_lo, mat_hi, fwd_snap[0], src
    )
    summed = scatter_rows(weighted, "shots", 1)
    grad_vel = 2.0 * density * velocity * summed / (4.0 * groups)
    return (current[None], older[None], grad_vel)


def solution(mesh):
    in_specs = (
        P("shots", "depth", None, None),
        P("shots", "depth", None, None),
        P("shots", None, "depth", None, None),
        P("depth", "shots", None),
        P("depth", "shots", None),
        P("shots"),
        P("shots", None),
        P("shots", None),
        P("shots", None, None),
    )
    out_specs = (
        P("shots", "depth", None, None),
        P("shots", "depth", None, None),
        P("depth", "shots", None),
    )
    return jax.shard_map(body, mesh=mesh, in_specs=in_specs, out_specs=out_specs, check_vma=False)
```
